256 devices in a mesh: ctx: 16 (over z, core), head: 16 (over y, x).
Axes of the slice: x: 4, y: 4, z: 8, core: 2. Of those that a mesh axis runs over, the one named last changes fastest.
Arguments:
- x_proj: bfloat16 [8192, 8192], P('ctx', 'head'), may hold values from -6 to 6
- z_proj: bfloat16 [8192, 8192], P('ctx', 'head'), may hold values from -6 to 6
- b_proj: bfloat16 [8192, 128], P('ctx'), may hold values from -6 to 6
- c_proj: bfloat16 [8192, 128], P('ctx'), may hold values from -6 to 6
- dt_raw: float32 [128, 8192], P('head', 'ctx'), may hold values from -6 to -2
- a_log: float32 [128], P('head'), may hold values from -11 to 4
- d_skip: float32 [128], P('head'), may hold values from 0.5 to 2
- conv_x: float32 [4, 8192], P(None, 'head'), may hold values from -3 to 3
- conv_bc: float32 [4, 256], replicated, may hold values from -3 to 3
- norm_gain: float32 [8192], P('head'), may hold values from 0.5 to 1.5
- grad_out: bfloat16 [8192, 8192], P('ctx', 'head'), may hold values from -6 to 6
Outputs:
- y_out: bfloat16 [8192, 8192], P('ctx', 'head')
- grad_x: bfloat16 [8192, 8192], P('ctx', 'head')
- grad_z: bfloat16 [8192, 8192], P('ctx', 'head')
- grad_b: bfloat16 [8192, 128], P(('ctx', 'head'))
- grad_c: bfloat16 [8192, 128], P(('ctx', 'head'))
- grad_dt: float32 [128, 8192], P('head', 'ctx')
- grad_alog: float32 [128], P('head')
- grad_dskip: float32 [128], P('head')
- grad_convx: float32 [4, 8192], P(None, 'head')
- grad_convbc: float32 [4, 256], replicated
- grad_gain: float32 [8192], P('head')
The draws below stay inside these ranges and needn't reach their ends.
All inputs are finite; a program needn't handle non-finite values.
Results may differ from the reference program's by a relative error of at most 0.023.
Values may be sent and summed in bfloat16 or wider, within the bound.
No kernel may reach another device: no remote copies, remote signals or barrier semaphores. Data moves between devices by JAX's collectives and lax.ppermute only.
A program may use at most 64 MiB of HBM per device.

```python
import jax
import jax.numpy as jnp
from jax import lax

HEADS = 128
HEAD_DIM = 64
STATE = 128
GROUP = 256
KERNEL = 4
TOK_DEV = 512
TOKENS = 8192


def head_rates(key):
    ranking = jax.random.permutation(jax.random.fold_in(key, 101), HEADS)
    slow_count = HEADS // 2
    is_slow = ranking < slow_count
    spread = jax.random.uniform(jax.random.fold_in(key, 102), (HEADS,), jnp.float32)
    slow_rate = (0.05 + 0.2 * spread) / TOKENS
    fast_rate = (5.0 + 3.0 * spread) / GROUP
    return jnp.where(is_slow, slow_rate, fast_rate) / 0.02


def draw_a_log(key, part):
    return jnp.log(head_rates(key))


def draw_dt_raw(key, part):
    rough_key = jax.random.fold_in(key, 103)
    step_size = jnp.exp(jax.random.uniform(rough_key, (HEADS, TOKENS), jnp.float32, jnp.log(0.01), jnp.log(0.04)))
    factor = jnp.exp(jax.random.uniform(jax.random.fold_in(key, 104), (HEADS, TOKENS // TOK_DEV), jnp.float32, -0.7, 0.7))
    step_size = step_size * jnp.repeat(factor, TOK_DEV, axis=1)
    return jnp.log(jnp.expm1(step_size))


def strengthened(result, own_key, source, target, blocks, factor):
    owner, partner = [(jnp.arange(result.shape[dim]) // (result.shape[dim] // blocks)).reshape([-1 if axis == dim else 1 for axis in range(result.ndim)]) for dim in (source, target)]
    chosen = jax.random.permutation(own_key, blocks)[partner]
    strong = (owner == chosen) | (owner == (partner + blocks // 2) % blocks)
    return jnp.where(strong, factor * result, result)


def levels(key, shape, split, least, top_value):
    def one(position, blocks):
        draws = jax.random.uniform(jax.random.fold_in(jax.random.fold_in(key, 6), position), (blocks,), jnp.float32, least / len(split), top_value / len(split))
        return jnp.repeat(jnp.exp(draws), shape[position] // blocks).reshape((-1,) + (1,) * (len(shape) - position - 1))

    loudness = one(*split[0])
    for cut in split[1:]:
        loudness = loudness * one(*cut)
    return loudness


def centred(rng, extent, width, bound, cuts=(), held_as=jnp.bfloat16):
    factor_of = levels(rng, extent, cuts, -0.22, 0.18) if cuts else 1.0
    drawn = jax.random.normal(rng, extent, jnp.float32) * width * factor_of
    return jnp.minimum(jnp.maximum(drawn, -bound), bound).astype(held_as)


def noise_with(stream_key, dims, width, bound, shards, heavy, kind=jnp.bfloat16):
    values = width * jax.random.normal(stream_key, dims, jnp.float32)
    if shards:
        values = values * levels(stream_key, dims, shards, -0.22, 0.18)
    return jnp.clip(strengthened(values, jax.random.fold_in(stream_key, 3), *heavy), -bound, bound).astype(kind)


def setup_inputs(seed: int = 0) -> dict:
    splits = jax.random.split(jax.random.key(seed), 12)
    return {
        "x_proj": centred(splits[0], (TOKENS, HEADS * HEAD_DIM), 1.0, 6.0, ((0, 16), (1, 16))),
        "z_proj": centred(splits[1], (TOKENS, HEADS * HEAD_DIM), 1.0, 6.0, ((0, 16), (1, 16))),
        "b_proj": centred(splits[2], (TOKENS, STATE), 1.0, 6.0, ((0, 16),)),
        "c_proj": centred(splits[3], (TOKENS, STATE), 1.0, 6.0, ((0, 16),)),
        "dt_raw": draw_dt_raw(jax.random.fold_in(splits[11], 71), 0),
        "a_log": draw_a_log(jax.random.fold_in(splits[11], 71), 0),
        "d_skip": jnp.clip(0.5 + 1.5 * jax.random.uniform(splits[6], (HEADS,), jnp.float32) ** levels(splits[6], (HEADS,), ((0, 16),), -0.2, 0.2), 0.5, 2.0),
        "conv_x": centred(splits[7], (KERNEL, HEADS * HEAD_DIM), KERNEL ** -0.5, 3.0, ((1, 16),), jnp.float32),
        "conv_bc": centred(splits[8], (KERNEL, 2 * STATE), KERNEL ** -0.5, 3.0, (), jnp.float32),
        "norm_gain": jnp.clip(0.5 + 1.0 * jax.random.uniform(splits[9], (HEADS * HEAD_DIM,), jnp.float32) ** levels(splits[9], (HEADS * HEAD_DIM,), ((0, 16),), -0.2, 0.2), 0.5, 1.5),
        "grad_out": noise_with(splits[10], (TOKENS, HEADS * HEAD_DIM), 1.0, 6.0, ((0, 16), (1, 16)), (1, 0, 16, 2.0)),
    }


HIGH = lax.Precision.HIGHEST
EPS = 1e-05

def tap_sum(padded, weight, count):
    summed = jnp.zeros((count, padded.shape[1]), jnp.float32)
    for offset in range(weight.shape[0]):
        summed = summed + weight[offset][None, :] * padded[offset:offset + count]
    return summed

def decay_table(cum_here):
    size_rows = cum_here.shape[0]
    row_ids = lax.broadcasted_iota(jnp.int32, (size_rows, size_rows), 0)
    col_ids = lax.broadcasted_iota(jnp.int32, (size_rows, size_rows), 1)
    allowed = (col_ids <= row_ids)[:, :, None]
    spread = cum_here[:, None, :] - cum_here[None, :, :]
    return jnp.where(allowed, jnp.exp(jnp.where(allowed, spread, 0.0)), 0.0)

def forward(x_in, z_in, b_in, c_in, dt_in, a_log, d_skip, conv_x, conv_bc, norm_gain):
    decay_rate = jnp.exp(a_log)
    blocks = TOKENS // GROUP
    lag_rows = KERNEL - 1
    bc_in = jnp.concatenate([b_in, c_in], axis=1)
    x_seq = x_in.reshape(blocks, GROUP, HEADS * HEAD_DIM)
    z_seq = z_in.reshape(blocks, GROUP, HEADS * HEAD_DIM)
    bc_seq = bc_in.reshape(blocks, GROUP, 2 * STATE)
    dt_seq = dt_in.T.reshape(blocks, GROUP, HEADS)

    def advance(carry_in, inputs):
        running, x_tail, bc_tail = carry_in
        x_raw, z_raw, bc_raw, dt_here = inputs
        x_full = jnp.concatenate([x_tail, x_raw], axis=0)
        bc_full = jnp.concatenate([bc_tail, bc_raw], axis=0)
        x_act = jax.nn.silu(tap_sum(x_full, conv_x, GROUP))
        bc_act = jax.nn.silu(tap_sum(bc_full, conv_bc, GROUP))
        b_act = bc_act[:, :STATE]
        c_act = bc_act[:, STATE:]
        step_size = jax.nn.softplus(dt_here)
        cum_here = jnp.cumsum(-step_size * decay_rate[None, :], axis=0)
        x_heads = x_act.reshape(GROUP, HEADS, HEAD_DIM)
        decay_map = decay_table(cum_here)
        scores = jnp.dot(c_act, b_act.T, precision=HIGH)
        mixing = scores[:, :, None] * decay_map * step_size[None, :, :]
        inside = jnp.einsum('tsh,shp->thp', mixing, x_heads, precision=HIGH)
        carried = jnp.exp(cum_here)[:, :, None] * jnp.einsum('tn,hpn->thp', c_act, running, precision=HIGH)
        ssm_out = (inside + carried + d_skip[None, :, None] * x_heads).reshape(GROUP, HEADS * HEAD_DIM)
        tail_decay = jnp.exp(cum_here[-1:, :] - cum_here) * step_size
        updated = jnp.exp(cum_here[-1])[:, None, None] * running + jnp.einsum('shp,sn->hpn', tail_decay[:, :, None] * x_heads, b_act, precision=HIGH)
        gated_out = ssm_out * jax.nn.silu(z_raw)
        inv_rms = lax.rsqrt(lax.optimization_barrier(jnp.mean(gated_out * gated_out, axis=1, keepdims=True)) + EPS)
        normed = gated_out * inv_rms * norm_gain[None, :]
        return ((updated, x_raw[GROUP - lag_rows:], bc_raw[GROUP - lag_rows:]), normed)
    advance = jax.checkpoint(advance)
    start = (jnp.zeros((HEADS, HEAD_DIM, STATE), jnp.float32), jnp.zeros((lag_rows, HEADS * HEAD_DIM), jnp.float32), jnp.zeros((lag_rows, 2 * STATE), jnp.float32))
    _, normed_blocks = lax.scan(advance, start, (x_seq, z_seq, bc_seq, dt_seq))
    return normed_blocks.reshape(TOKENS, HEADS * HEAD_DIM)

def reference(x_proj, z_proj, b_proj, c_proj, dt_raw, a_log, d_skip, conv_x, conv_bc, norm_gain, grad_out):
    primals = (x_proj.astype(jnp.float32), z_proj.astype(jnp.float32), b_proj.astype(jnp.float32), c_proj.astype(jnp.float32), dt_raw, a_log, d_skip, conv_x, conv_bc, norm_gain)
    normed, pullback = jax.vjp(forward, *primals)
    gradients = pullback(grad_out.astype(jnp.float32))
    return (normed.astype(jnp.bfloat16), gradients[0].astype(jnp.bfloat16), gradients[1].astype(jnp.bfloat16), gradients[2].astype(jnp.bfloat16), gradients[3].astype(jnp.bfloat16), gradients[4], gradients[5], gradients[6], gradients[7], gradients[8], gradients[9])
```

```python
import jax
import jax.numpy as jnp
from jax import lax
from jax.sharding import PartitionSpec as P

HEADS = 128
HEAD_DIM = 64
GROUP = 256


HIGH = lax.Precision.HIGHEST
EPS = 1e-05


def passed_along(block, axis, distance):
    devices = range(lax.axis_size(axis))
    route = [(i - distance, i) for i in devices if i - distance in devices]
    return lax.ppermute(block, axis, route)


def exclusive_scan(decay, state, axis, direction):
    count = lax.axis_size(axis)
    inc_decay, inc_state = decay, state
    exc_decay = jnp.ones_like(decay)
    exc_state = jnp.zeros_like(state)
    distance = 1
    while distance < count:
        got_decay, got_state = passed_along((inc_decay, inc_state), axis, distance * direction)
        exc_state = exc_decay[:, None, None] * got_state + exc_state
        exc_decay = exc_decay * got_decay
        if 2 * distance < count:
            inc_state = inc_decay[:, None, None] * got_state + inc_state
            inc_decay = inc_decay * got_decay
        distance *= 2
    return exc_state


def silu_grad(value):
    sigma = jax.nn.sigmoid(value)
    return sigma * (1.0 + value * (1.0 - sigma))


def tap_sum(padded, weight, count):
    summed = jnp.zeros((count, padded.shape[1]), jnp.float32)
    for offset in range(weight.shape[0]):
        summed = summed + weight[offset][None, :] * padded[offset : offset + count].astype(
            jnp.float32
        )
    return summed


def back_taps(ahead, weight, count):
    final_tap = weight.shape[0] - 1
    summed = jnp.zeros((count, ahead.shape[1]), jnp.float32)
    for offset in range(weight.shape[0]):
        summed = (
            summed
            + weight[offset][None, :] * ahead[final_tap - offset : final_tap - offset + count]
        )
    return summed


def weight_taps(grad_pre, padded, count, tap_count):
    return jnp.stack(
        [
            jnp.sum(grad_pre * padded[offset : offset + count].astype(jnp.float32), axis=0)
            for offset in range(tap_count)
        ]
    )


def decay_table(cum_blocks):
    size_rows = cum_blocks.shape[1]
    row_ids = lax.broadcasted_iota(jnp.int32, (size_rows, size_rows), 0)
    col_ids = lax.broadcasted_iota(jnp.int32, (size_rows, size_rows), 1)
    allowed = (col_ids <= row_ids)[None, :, :, None]
    spread = cum_blocks[:, :, None, :] - cum_blocks[:, None, :, :]
    return jnp.where(allowed, jnp.exp(jnp.where(allowed, spread, 0.0)), 0.0)


def local(
    x_proj, z_proj, b_proj, c_proj, dt_raw, a_log, d_skip, conv_x, conv_bc, norm_gain, grad_out
):
    length = x_proj.shape[0]
    head_count = dt_raw.shape[0]
    row_width = x_proj.shape[1]
    head_dim = row_width // head_count
    state_dim = b_proj.shape[1]
    tap_count = conv_x.shape[0]
    blocks = length // GROUP
    channels = HEADS * HEAD_DIM
    bc_proj = jnp.concatenate([b_proj, c_proj], axis=1)
    edges = passed_along(
        (x_proj[length - tap_count + 1 :], bc_proj[length - tap_count + 1 :]), "ctx", 1
    )
    x_padded = jnp.concatenate([edges[0], x_proj], axis=0)
    bc_padded = jnp.concatenate([edges[1], bc_proj], axis=0)
    x_pre = tap_sum(x_padded, conv_x, length)
    bc_pre = tap_sum(bc_padded, conv_bc, length)
    x_act = jax.nn.silu(x_pre)
    bc_act = jax.nn.silu(bc_pre)
    decay_rate = jnp.exp(a_log)
    step_size = jax.nn.softplus(dt_raw).T
    x_blocks = x_act.reshape(blocks, GROUP, head_count, head_dim)
    b_blocks = bc_act[:, :state_dim].reshape(blocks, GROUP, state_dim)
    c_blocks = bc_act[:, state_dim:].reshape(blocks, GROUP, state_dim)
    d_blocks = step_size.reshape(blocks, GROUP, head_count)
    cum_blocks = jnp.cumsum(
        (-step_size * decay_rate[None, :]).reshape(blocks, GROUP, head_count), axis=1
    )
    block_ends = cum_blocks[:, -1, :]
    block_decay = jnp.exp(block_ends)
    tail_decay = jnp.exp(cum_blocks[:, -1:, :] - cum_blocks)
    tail_weight = tail_decay * d_blocks
    block_states = jnp.einsum(
        "cshp,csn->chpn", tail_weight[..., None] * x_blocks, b_blocks, precision=HIGH
    )

    running = jnp.zeros((head_count, head_dim, state_dim), jnp.float32)
    local_entering = []
    for index in range(blocks):
        local_entering.append(running)
        running = block_decay[index][:, None, None] * running + block_states[index]
    shard_state = running
    local_entering = jnp.stack(local_entering)
    prefix_log = jnp.cumsum(block_ends, axis=0) - block_ends
    shard_decay = jnp.exp(jnp.sum(block_ends, axis=0))

    entering = exclusive_scan(shard_decay, shard_state, "ctx", 1)
    block_entry = jnp.exp(prefix_log)[:, :, None, None] * entering[None] + local_entering

    decay_map = decay_table(cum_blocks)
    scores = jnp.einsum("ctn,csn->cts", c_blocks, b_blocks, precision=HIGH)
    weighted = scores[..., None] * decay_map
    mixing = weighted * d_blocks[:, None, :, :]
    inside = jnp.einsum("ctsh,cshp->cthp", mixing, x_blocks, precision=HIGH)
    carried_raw = jnp.einsum("ctn,chpn->cthp", c_blocks, block_entry, precision=HIGH)
    start_decay = jnp.exp(cum_blocks)
    ssm_blocks = inside + start_decay[..., None] * carried_raw
    skip_rep = jnp.repeat(d_skip, head_dim)
    ssm_out = ssm_blocks.reshape(length, row_width) + skip_rep[None, :] * x_act
    z_float = z_proj.astype(jnp.float32)
    gate_act = jax.nn.silu(z_float)
    gated_out = ssm_out * gate_act
    grad_float = grad_out.astype(jnp.float32)
    scaled_grad = norm_gain[None, :] * grad_float
    norm_sums = lax.psum(
        jnp.stack(
            [jnp.sum(gated_out * gated_out, axis=1), jnp.sum(scaled_grad * gated_out, axis=1)]
        ),
        "head",
    )
    square_sum, cross_sum = norm_sums[0], norm_sums[1]
    inv_rms = lax.rsqrt(square_sum / channels + EPS)[:, None]
    y_out = (gated_out * inv_rms * norm_gain[None, :]).astype(jnp.bfloat16)
    grad_gain_part = jnp.sum(grad_float * gated_out * inv_rms, axis=0)
    grad_gated = inv_rms * scaled_grad - gated_out * (inv_rms * inv_rms * inv_rms) * (
        cross_sum[:, None] / channels
    )
    grad_ssm = grad_gated * gate_act
    grad_z = (grad_gated * ssm_out * silu_grad(z_float)).astype(jnp.bfloat16)
    grad_skip_part = jnp.sum((grad_ssm * x_act).reshape(length, head_count, head_dim), axis=(0, 2))
    grad_blocks = grad_ssm.reshape(blocks, GROUP, head_count, head_dim)
    start_map = start_decay[..., None] * grad_blocks
    local_pull = jnp.einsum("cthp,ctn->chpn", start_map, c_blocks, precision=HIGH)
    shard_pull = jnp.sum(jnp.exp(prefix_log)[:, :, None, None] * local_pull, axis=0)

    leaving = exclusive_scan(shard_decay, shard_pull, "ctx", -1)
    running = leaving
    block_exit = [None] * blocks
    for index in reversed(range(blocks)):
        block_exit[index] = running
        running = block_decay[index][:, None, None] * running + local_pull[index]
    block_exit = jnp.stack(block_exit)

    b_exit = jnp.einsum("csn,chpn->cshp", b_blocks, block_exit, precision=HIGH)
    pulled = (
        jnp.einsum("ctsh,cthp->cshp", weighted, grad_blocks, precision=HIGH)
        + tail_decay[..., None] * b_exit
    )
    grad_x_blocks = d_blocks[..., None] * pulled
    grad_step_blocks = jnp.sum(x_blocks * pulled, axis=3)
    pair_grad = jnp.einsum("cthp,cshp->ctsh", grad_blocks, x_blocks, precision=HIGH)
    masked = pair_grad * decay_map * d_blocks[:, None, :, :]
    grad_scores = jnp.sum(masked, axis=3)
    grad_c_blocks = jnp.einsum("cts,csn->ctn", grad_scores, b_blocks, precision=HIGH)
    grad_b_blocks = jnp.einsum("cts,ctn->csn", grad_scores, c_blocks, precision=HIGH)
    through = masked * scores[..., None]
    grad_cum = jnp.sum(through, axis=2) - jnp.sum(through, axis=1)
    grad_cum = grad_cum + jnp.sum(start_map * carried_raw, axis=3)
    grad_c_blocks = grad_c_blocks + jnp.einsum(
        "cthp,chpn->ctn", start_map, block_entry, precision=HIGH
    )
    release = tail_weight * jnp.sum(x_blocks * b_exit, axis=3)
    grad_cum = grad_cum - release
    end_total = jnp.sum(release, axis=1) + jnp.exp(block_ends) * jnp.sum(
        block_entry * block_exit, axis=(2, 3)
    )
    grad_cum = jnp.concatenate(
        [grad_cum[:, :-1], grad_cum[:, -1:] + end_total[:, None, :]], axis=1
    )
    grad_log_blocks = jnp.flip(jnp.cumsum(jnp.flip(grad_cum, 1), axis=1), 1)
    grad_b_blocks = grad_b_blocks + jnp.einsum(
        "cshp,chpn->csn", tail_weight[..., None] * x_blocks, block_exit, precision=HIGH
    )

    grad_log_rows = grad_log_blocks.reshape(length, head_count)
    grad_step_rows = (
        grad_step_blocks.reshape(length, head_count) - decay_rate[None, :] * grad_log_rows
    )
    grad_alog_part = decay_rate * -jnp.sum(step_size * grad_log_rows, axis=0)
    grad_dt = (grad_step_rows * jax.nn.sigmoid(dt_raw).T).T
    grad_x_act = grad_x_blocks.reshape(length, row_width) + skip_rep[None, :] * grad_ssm
    grad_bc_act = jnp.concatenate(
        [grad_b_blocks.reshape(length, state_dim), grad_c_blocks.reshape(length, state_dim)], axis=1
    )
    grad_x_pre = grad_x_act * silu_grad(x_pre)
    grad_bc_pre = grad_bc_act * silu_grad(bc_pre)
    ahead = passed_along((grad_x_pre[: tap_count - 1], grad_bc_pre[: tap_count - 1]), "ctx", -1)
    x_ahead = jnp.concatenate([grad_x_pre, ahead[0]], axis=0)
    bc_ahead = jnp.concatenate([grad_bc_pre, ahead[1]], axis=0)
    grad_x = back_taps(x_ahead, conv_x, length).astype(jnp.bfloat16)
    bc_back = back_taps(bc_ahead, conv_bc, length)
    shares = lax.psum_scatter(bc_back, "head", scatter_dimension=0, tiled=True)
    grad_b = shares[:, :state_dim].astype(jnp.bfloat16)
    grad_c = shares[:, state_dim:].astype(jnp.bfloat16)
    grad_convx_part = weight_taps(grad_x_pre, x_padded, length, tap_count)
    grad_convbc_part = weight_taps(grad_bc_pre, bc_padded, length, tap_count)

    head_slots = lax.axis_size("head")
    own_slot = lax.axis_index("head")
    per_head = jnp.concatenate(
        [grad_alog_part, grad_skip_part, grad_convx_part.reshape(-1), grad_gain_part]
    )
    slot_mask = (jnp.arange(head_slots) == own_slot).astype(jnp.float32)[:, None]
    slots = (slot_mask * per_head[None, :]).reshape(-1)
    totals = lax.psum(jnp.concatenate([slots, grad_convbc_part.reshape(-1)]), ("ctx", "head"))
    per_size = per_head.shape[0]
    own_total = lax.dynamic_slice_in_dim(totals, own_slot * per_size, per_size)
    grad_alog = own_total[:head_count]
    grad_dskip = own_total[head_count : 2 * head_count]
    convx_size = grad_convx_part.size
    grad_convx = own_total[2 * head_count : 2 * head_count + convx_size].reshape(
        grad_convx_part.shape
    )
    grad_gain = own_total[2 * head_count + convx_size :]
    grad_convbc = totals[head_slots * per_size :].reshape(grad_convbc_part.shape)
    return (
        y_out,
        grad_x,
        grad_z,
        grad_b,
        grad_c,
        grad_dt,
        grad_alog,
        grad_dskip,
        grad_convx,
        grad_convbc,
        grad_gain,
    )


def solution(mesh):
    return jax.shard_map(
        local,
        mesh=mesh,
        in_specs=(
            P("ctx", "head"),
            P("ctx", "head"),
            P("ctx", None),
            P("ctx", None),
            P("head", "ctx"),
            P("head"),
            P("head"),
            P(None, "head"),
            P(),
            P("head"),
            P("ctx", "head"),
        ),
        out_specs=(
            P("ctx", "head"),
            P("ctx", "head"),
            P("ctx", "head"),
            P(("ctx", "head"), None),
            P(("ctx", "head"), None),
            P("head", "ctx"),
            P("head"),
            P("head"),
            P(None, "head"),
            P(),
            P("head"),
        ),
        check_vma=False,
    )
```

```python
import jax
import jax.numpy as jnp
from jax import lax
from jax.sharding import PartitionSpec as P

HEADS = 128
HEAD_DIM = 64
GROUP = 256


HIGH = lax.Precision.HIGHEST
EPS = 1e-05


def passed_along(block, axis, distance):
    devices = range(lax.axis_size(axis))
    route = [(i - distance, i) for i in devices if i - distance in devices]
    return lax.ppermute(block, axis, route)


def exclusive_scan(decay, state, axis, direction):
    count = lax.axis_size(axis)
    inc_decay, inc_state = decay, state
    exc_decay = jnp.ones_like(decay)
    exc_state = jnp.zeros_like(state)
    distance = 1
    while distance < count:
        got_decay, got_state = passed_along((inc_decay, inc_state), axis, distance * direction)
        exc_state = exc_decay[:, None, None] * got_state + exc_state
        exc_decay = exc_decay * got_decay
        if 2 * distance < count:
            inc_state = inc_decay[:, None, None] * got_state + inc_state
            inc_decay = inc_decay * got_decay
        distance *= 2
    return exc_state


def digit_plan(count):
    plan = []
    stride = 1
    while stride < count:
        radix = 4 if (count // stride) % 4 == 0 else 2
        plan.append((stride, radix))
        stride *= radix
    return plan


def shifted(block, axis, stride, radix, shift):
    route = []
    for source in range(lax.axis_size(axis)):
        digit = (source // stride) % radix
        route.append((source, source + ((digit + shift) % radix - digit) * stride))
    return lax.ppermute(block, axis, route)


def all_sum(block, axis):
    for stride, radix in digit_plan(lax.axis_size(axis)):
        got = [block] + [shifted(block, axis, stride, radix, shift) for shift in range(1, radix)]
        digit = (lax.axis_index(axis) // stride) % radix
        ordered = jnp.take(jnp.stack(got), (digit - jnp.arange(radix)) % radix, axis=0)
        block = ordered[0]
        for index in range(1, radix):
            block = block + ordered[index]
    return block


def sum_scatter(block, axis):
    count = lax.axis_size(axis)
    plan = digit_plan(count)
    trailing = block.ndim - 1
    chunk = block.shape[0] // count
    block = block.reshape(tuple(radix for _, radix in reversed(plan)) + (chunk,) + block.shape[1:])
    for stride, radix in plan:
        digit = (lax.axis_index(axis) // stride) % radix
        where = block.ndim - 2 - trailing
        total = lax.dynamic_index_in_dim(block, digit, axis=where, keepdims=False)
        for shift in range(1, radix):
            part = lax.dynamic_index_in_dim(block, (digit + shift) % radix, axis=where, keepdims=False)
            total = total + shifted(part, axis, stride, radix, shift)
        block = total
    return block


def silu_grad(value):
    sigma = jax.nn.sigmoid(value)
    return sigma * (1.0 + value * (1.0 - sigma))


def tap_sum(padded, weight, count):
    summed = jnp.zeros((count, padded.shape[1]), jnp.float32)
    for offset in range(weight.shape[0]):
        summed = summed + weight[offset][None, :] * padded[offset : offset + count].astype(
            jnp.float32
        )
    return summed


def back_taps(ahead, weight, count):
    final_tap = weight.shape[0] - 1
    summed = jnp.zeros((count, ahead.shape[1]), jnp.float32)
    for offset in range(weight.shape[0]):
        summed = (
            summed
            + weight[offset][None, :] * ahead[final_tap - offset : final_tap - offset + count]
        )
    return summed


def weight_taps(grad_pre, padded, count, tap_count):
    return jnp.stack(
        [
            jnp.sum(grad_pre * padded[offset : offset + count].astype(jnp.float32), axis=0)
            for offset in range(tap_count)
        ]
    )


def decay_table(cum_blocks):
    size_rows = cum_blocks.shape[1]
    row_ids = lax.broadcasted_iota(jnp.int32, (size_rows, size_rows), 0)
    col_ids = lax.broadcasted_iota(jnp.int32, (size_rows, size_rows), 1)
    allowed = (col_ids <= row_ids)[None, :, :, None]
    spread = cum_blocks[:, :, None, :] - cum_blocks[:, None, :, :]
    return jnp.where(allowed, jnp.exp(jnp.where(allowed, spread, 0.0)), 0.0)


def local(
    x_proj, z_proj, b_proj, c_proj, dt_raw, a_log, d_skip, conv_x, conv_bc, norm_gain, grad_out
):
    length = x_proj.shape[0]
    head_count = dt_raw.shape[0]
    row_width = x_proj.shape[1]
    head_dim = row_width // head_count
    state_dim = b_proj.shape[1]
    tap_count = conv_x.shape[0]
    blocks = length // GROUP
    channels = HEADS * HEAD_DIM
    bc_proj = jnp.concatenate([b_proj, c_proj], axis=1)
    edges = passed_along(
        (x_proj[length - tap_count + 1 :], bc_proj[length - tap_count + 1 :]), "ctx", 1
    )
    x_padded = jnp.concatenate([edges[0], x_proj], axis=0)
    bc_padded = jnp.concatenate([edges[1], bc_proj], axis=0)
    x_pre = tap_sum(x_padded, conv_x, length)
    bc_pre = tap_sum(bc_padded, conv_bc, length)
    x_act = jax.nn.silu(x_pre)
    bc_act = jax.nn.silu(bc_pre)
    decay_rate = jnp.exp(a_log)
    step_size = jax.nn.softplus(dt_raw).T
    x_blocks = x_act.reshape(blocks, GROUP, head_count, head_dim)
    b_blocks = bc_act[:, :state_dim].reshape(blocks, GROUP, state_dim)
    c_blocks = bc_act[:, state_dim:].reshape(blocks, GROUP, state_dim)
    d_blocks = step_size.reshape(blocks, GROUP, head_count)
    cum_blocks = jnp.cumsum(
        (-step_size * decay_rate[None, :]).reshape(blocks, GROUP, head_count), axis=1
    )
    block_ends = cum_blocks[:, -1, :]
    block_decay = jnp.exp(block_ends)
    tail_decay = jnp.exp(cum_blocks[:, -1:, :] - cum_blocks)
    tail_weight = tail_decay * d_blocks
    block_states = jnp.einsum(
        "cshp,csn->chpn", tail_weight[..., None] * x_blocks, b_blocks, precision=HIGH
    )

    running = jnp.zeros((head_count, head_dim, state_dim), jnp.float32)
    local_entering = []
    for index in range(blocks):
        local_entering.append(running)
        running = block_decay[index][:, None, None] * running + block_states[index]
    shard_state = running
    local_entering = jnp.stack(local_entering)
    prefix_log = jnp.cumsum(block_ends, axis=0) - block_ends
    shard_decay = jnp.exp(jnp.sum(block_ends, axis=0))

    entering = exclusive_scan(shard_decay, shard_state, "ctx", 1)
    block_entry = jnp.exp(prefix_log)[:, :, None, None] * entering[None] + local_entering

    decay_map = decay_table(cum_blocks)
    scores = jnp.einsum("ctn,csn->cts", c_blocks, b_blocks, precision=HIGH)
    weighted = scores[..., None] * decay_map
    mixing = weighted * d_blocks[:, None, :, :]
    inside = jnp.einsum("ctsh,cshp->cthp", mixing, x_blocks, precision=HIGH)
    carried_raw = jnp.einsum("ctn,chpn->cthp", c_blocks, block_entry, precision=HIGH)
    start_decay = jnp.exp(cum_blocks)
    ssm_blocks = inside + start_decay[..., None] * carried_raw
    skip_rep = jnp.repeat(d_skip, head_dim)
    ssm_out = ssm_blocks.reshape(length, row_width) + skip_rep[None, :] * x_act
    z_float = z_proj.astype(jnp.float32)
    gate_act = jax.nn.silu(z_float)
    gated_out = ssm_out * gate_act
    grad_float = grad_out.astype(jnp.float32)
    scaled_grad = norm_gain[None, :] * grad_float
    norm_sums = all_sum(
        jnp.stack(
            [jnp.sum(gated_out * gated_out, axis=1), jnp.sum(scaled_grad * gated_out, axis=1)]
        ),
        "head",
    )
    square_sum, cross_sum = norm_sums[0], norm_sums[1]
    inv_rms = lax.rsqrt(square_sum / channels + EPS)[:, None]
    y_out = (gated_out * inv_rms * norm_gain[None, :]).astype(jnp.bfloat16)
    grad_gain_part = jnp.sum(grad_float * gated_out * inv_rms, axis=0)
    grad_gated = inv_rms * scaled_grad - gated_out * (inv_rms * inv_rms * inv_rms) * (
        cross_sum[:, None] / channels
    )
    grad_ssm = grad_gated * gate_act
    grad_z = (grad_gated * ssm_out * silu_grad(z_float)).astype(jnp.bfloat16)
    grad_skip_part = jnp.sum((grad_ssm * x_act).reshape(length, head_count, head_dim), axis=(0, 2))
    grad_blocks = grad_ssm.reshape(blocks, GROUP, head_count, head_dim)
    start_map = start_decay[..., None] * grad_blocks
    local_pull = jnp.einsum("cthp,ctn->chpn", start_map, c_blocks, precision=HIGH)
    shard_pull = jnp.sum(jnp.exp(prefix_log)[:, :, None, None] * local_pull, axis=0)

    leaving = exclusive_scan(shard_decay, shard_pull, "ctx", -1)
    running = leaving
    block_exit = [None] * blocks
    for index in reversed(range(blocks)):
        block_exit[index] = running
        running = block_decay[index][:, None, None] * running + local_pull[index]
    block_exit = jnp.stack(block_exit)

    b_exit = jnp.einsum("csn,chpn->cshp", b_blocks, block_exit, precision=HIGH)
    pulled = (
        jnp.einsum("ctsh,cthp->cshp", weighted, grad_blocks, precision=HIGH)
        + tail_decay[..., None] * b_exit
    )
    grad_x_blocks = d_blocks[..., None] * pulled
    grad_step_blocks = jnp.sum(x_blocks * pulled, axis=3)
    pair_grad = jnp.einsum("cthp,cshp->ctsh", grad_blocks, x_blocks, precision=HIGH)
    masked = pair_grad * decay_map * d_blocks[:, None, :, :]
    grad_scores = jnp.sum(masked, axis=3)
    grad_c_blocks = jnp.einsum("cts,csn->ctn", grad_scores, b_blocks, precision=HIGH)
    grad_b_blocks = jnp.einsum("cts,ctn->csn", grad_scores, c_blocks, precision=HIGH)
    through = masked * scores[..., None]
    grad_cum = jnp.sum(through, axis=2) - jnp.sum(through, axis=1)
    grad_cum = grad_cum + jnp.sum(start_map * carried_raw, axis=3)
    grad_c_blocks = grad_c_blocks + jnp.einsum(
        "cthp,chpn->ctn", start_map, block_entry, precision=HIGH
    )
    release = tail_weight * jnp.sum(x_blocks * b_exit, axis=3)
    grad_cum = grad_cum - release
    end_total = jnp.sum(release, axis=1) + jnp.exp(block_ends) * jnp.sum(
        block_entry * block_exit, axis=(2, 3)
    )
    grad_cum = jnp.concatenate(
        [grad_cum[:, :-1], grad_cum[:, -1:] + end_total[:, None, :]], axis=1
    )
    grad_log_blocks = jnp.flip(jnp.cumsum(jnp.flip(grad_cum, 1), axis=1), 1)
    grad_b_blocks = grad_b_blocks + jnp.einsum(
        "cshp,chpn->csn", tail_weight[..., None] * x_blocks, block_exit, precision=HIGH
    )

    grad_log_rows = grad_log_blocks.reshape(length, head_count)
    grad_step_rows = (
        grad_step_blocks.reshape(length, head_count) - decay_rate[None, :] * grad_log_rows
    )
    grad_alog_part = decay_rate * -jnp.sum(step_size * grad_log_rows, axis=0)
    grad_dt = (grad_step_rows * jax.nn.sigmoid(dt_raw).T).T
    grad_x_act = grad_x_blocks.reshape(length, row_width) + skip_rep[None, :] * grad_ssm
    grad_bc_act = jnp.concatenate(
        [grad_b_blocks.reshape(length, state_dim), grad_c_blocks.reshape(length, state_dim)], axis=1
    )
    grad_x_pre = grad_x_act * silu_grad(x_pre)
    grad_bc_pre = grad_bc_act * silu_grad(bc_pre)
    ahead = passed_along((grad_x_pre[: tap_count - 1], grad_bc_pre[: tap_count - 1]), "ctx", -1)
    x_ahead = jnp.concatenate([grad_x_pre, ahead[0]], axis=0)
    bc_ahead = jnp.concatenate([grad_bc_pre, ahead[1]], axis=0)
    grad_x = back_taps(x_ahead, conv_x, length).astype(jnp.bfloat16)
    bc_back = back_taps(bc_ahead, conv_bc, length)
    shares = sum_scatter(bc_back, "head")
    grad_b = shares[:, :state_dim].astype(jnp.bfloat16)
    grad_c = shares[:, state_dim:].astype(jnp.bfloat16)
    grad_convx_part = weight_taps(grad_x_pre, x_padded, length, tap_count)
    grad_convbc_part = weight_taps(grad_bc_pre, bc_padded, length, tap_count)
    per_head = jnp.concatenate(
        [grad_alog_part, grad_skip_part, grad_convx_part.reshape(-1), grad_gain_part]
    )
    totals = all_sum(jnp.concatenate([per_head, grad_convbc_part.reshape(-1)]), "ctx")
    per_size = per_head.shape[0]
    grad_alog = totals[:head_count]
    grad_dskip = totals[head_count : 2 * head_count]
    convx_size = grad_convx_part.size
    grad_convx = totals[2 * head_count : 2 * head_count + convx_size].reshape(
        grad_convx_part.shape
    )
    grad_gain = totals[2 * head_count + convx_size : per_size]
    grad_convbc = all_sum(totals[per_size:], "head").reshape(grad_convbc_part.shape)
    return (
        y_out,
        grad_x,
        grad_z,
        grad_b,
        grad_c,
        grad_dt,
        grad_alog,
        grad_dskip,
        grad_convx,
        grad_convbc,
        grad_gain,
    )


def solution(mesh):
    return jax.shard_map(
        local,
        mesh=mesh,
        in_specs=(
            P("ctx", "head"),
            P("ctx", "head"),
            P("ctx", None),
            P("ctx", None),
            P("head", "ctx"),
            P("head"),
            P("head"),
            P(None, "head"),
            P(),
            P("head"),
            P("ctx", "head"),
        ),
        out_specs=(
            P("ctx", "head"),
            P("ctx", "head"),
            P("ctx", "head"),
            P(("ctx", "head"), None),
            P(("ctx", "head"), None),
            P("head", "ctx"),
            P("head"),
            P("head"),
            P(None, "head"),
            P(),
            P("head"),
        ),
        check_vma=False,
    )
```

```python
import jax
import jax.numpy as jnp
from jax import lax
from jax.sharding import PartitionSpec as P

HEADS = 128
HEAD_DIM = 64
GROUP = 256


HIGH = lax.Precision.HIGHEST
EPS = 1e-05


def passed_along(block, axis, distance):
    devices = range(lax.axis_size(axis))
    route = [(i - distance, i) for i in devices if i - distance in devices]
    return lax.ppermute(block, axis, route)


def exclusive_scan(decay, state, axis, direction):
    rows = state.shape[1]
    def packed(decay_part, state_part):
        decay_row = jnp.broadcast_to(decay_part[:, None, None], state_part[:, :1].shape)
        return jnp.concatenate([state_part, decay_row], axis=1)

    inc_decay, inc_state = decay, state
    exc_decay = jnp.ones_like(decay)
    exc_state = jnp.zeros_like(state)
    plan = digit_plan(lax.axis_size(axis))
    for index, (stride, radix) in enumerate(plan):
        message = packed(inc_decay, inc_state)
        got = [
            passed_along(message, axis, stride * shift * direction) for shift in range(1, radix)
        ]
        for part in got:
            exc_state = exc_state + exc_decay[:, None, None] * part[:, :rows]
            exc_decay = exc_decay * part[:, rows, 0]
        if index + 1 < len(plan):
            for part in got:
                inc_state = inc_state + inc_decay[:, None, None] * part[:, :rows]
                inc_decay = inc_decay * part[:, rows, 0]
    return exc_state


def digit_plan(count):
    plan = []
    stride = 1
    while stride < count:
        radix = 4 if (count // stride) % 4 == 0 else 2
        plan.append((stride, radix))
        stride *= radix
    return plan


def shifted(block, axis, stride, radix, shift):
    route = []
    for source in range(lax.axis_size(axis)):
        digit = (source // stride) % radix
        route.append((source, source + ((digit + shift) % radix - digit) * stride))
    return lax.ppermute(block, axis, route)


def all_sum(block, axis):
    for stride, radix in digit_plan(lax.axis_size(axis)):
        got = [block] + [shifted(block, axis, stride, radix, shift) for shift in range(1, radix)]
        digit = (lax.axis_index(axis) // stride) % radix
        ordered = jnp.take(jnp.stack(got), (digit - jnp.arange(radix)) % radix, axis=0)
        block = ordered[0]
        for index in range(1, radix):
            block = block + ordered[index]
    return block


def sum_scatter(block, axis):
    count = lax.axis_size(axis)
    plan = digit_plan(count)
    trailing = block.ndim - 1
    chunk = block.shape[0] // count
    block = block.reshape(tuple(radix for _, radix in reversed(plan)) + (chunk,) + block.shape[1:])
    for stride, radix in plan:
        digit = (lax.axis_index(axis) // stride) % radix
        where = block.ndim - 2 - trailing
        total = lax.dynamic_index_in_dim(block, digit, axis=where, keepdims=False)
        for shift in range(1, radix):
            part = lax.dynamic_index_in_dim(block, (digit + shift) % radix, axis=where, keepdims=False)
            total = total + shifted(part, axis, stride, radix, shift)
        block = total
    return block


def silu_grad(value):
    sigma = jax.nn.sigmoid(value)
    return sigma * (1.0 + value * (1.0 - sigma))


def tap_sum(padded, weight, count):
    summed = jnp.zeros((count, padded.shape[1]), jnp.float32)
    for offset in range(weight.shape[0]):
        summed = summed + weight[offset][None, :] * padded[offset : offset + count].astype(
            jnp.float32
        )
    return summed


def back_taps(ahead, weight, count):
    final_tap = weight.shape[0] - 1
    summed = jnp.zeros((count, ahead.shape[1]), jnp.float32)
    for offset in range(weight.shape[0]):
        summed = (
            summed
            + weight[offset][None, :] * ahead[final_tap - offset : final_tap - offset + count]
        )
    return summed


def weight_taps(grad_pre, padded, count, tap_count):
    return jnp.stack(
        [
            jnp.sum(grad_pre * padded[offset : offset + count].astype(jnp.float32), axis=0)
            for offset in range(tap_count)
        ]
    )


def decay_table(cum_blocks):
    size_rows = cum_blocks.shape[1]
    row_ids = lax.broadcasted_iota(jnp.int32, (size_rows, size_rows), 0)
    col_ids = lax.broadcasted_iota(jnp.int32, (size_rows, size_rows), 1)
    allowed = (col_ids <= row_ids)[None, :, :, None]
    spread = cum_blocks[:, :, None, :] - cum_blocks[:, None, :, :]
    return jnp.where(allowed, jnp.exp(jnp.where(allowed, spread, 0.0)), 0.0)


def local(
    x_proj, z_proj, b_proj, c_proj, dt_raw, a_log, d_skip, conv_x, conv_bc, norm_gain, grad_out
):
    length = x_proj.shape[0]
    head_count = dt_raw.shape[0]
    row_width = x_proj.shape[1]
    head_dim = row_width // head_count
    state_dim = b_proj.shape[1]
    tap_count = conv_x.shape[0]
    blocks = length // GROUP
    channels = HEADS * HEAD_DIM
    bc_proj = jnp.concatenate([b_proj, c_proj], axis=1)
    edges = passed_along(
        jnp.concatenate(
            [x_proj[length - tap_count + 1 :], bc_proj[length - tap_count + 1 :]], axis=1
        ),
        "ctx",
        1,
    )
    x_padded = jnp.concatenate([edges[:, :row_width], x_proj], axis=0)
    bc_padded = jnp.concatenate([edges[:, row_width:], bc_proj], axis=0)
    x_pre = tap_sum(x_padded, conv_x, length)
    bc_pre = tap_sum(bc_padded, conv_bc, length)
    x_act = jax.nn.silu(x_pre)
    bc_act = jax.nn.silu(bc_pre)
    decay_rate = jnp.exp(a_log)
    step_size = jax.nn.softplus(dt_raw).T
    x_blocks = x_act.reshape(blocks, GROUP, head_count, head_dim)
    b_blocks = bc_act[:, :state_dim].reshape(blocks, GROUP, state_dim)
    c_blocks = bc_act[:, state_dim:].reshape(blocks, GROUP, state_dim)
    d_blocks = step_size.reshape(blocks, GROUP, head_count)
    cum_blocks = jnp.cumsum(
        (-step_size * decay_rate[None, :]).reshape(blocks, GROUP, head_count), axis=1
    )
    block_ends = cum_blocks[:, -1, :]
    block_decay = jnp.exp(block_ends)
    tail_decay = jnp.exp(cum_blocks[:, -1:, :] - cum_blocks)
    tail_weight = tail_decay * d_blocks
    block_states = jnp.einsum(
        "cshp,csn->chpn", tail_weight[..., None] * x_blocks, b_blocks, precision=HIGH
    )

    running = jnp.zeros((head_count, head_dim, state_dim), jnp.float32)
    local_entering = []
    for index in range(blocks):
        local_entering.append(running)
        running = block_decay[index][:, None, None] * running + block_states[index]
    shard_state = running
    local_entering = jnp.stack(local_entering)
    prefix_log = jnp.cumsum(block_ends, axis=0) - block_ends
    shard_decay = jnp.exp(jnp.sum(block_ends, axis=0))

    entering = exclusive_scan(shard_decay, shard_state, "ctx", 1)
    block_entry = jnp.exp(prefix_log)[:, :, None, None] * entering[None] + local_entering

    decay_map = decay_table(cum_blocks)
    scores = jnp.einsum("ctn,csn->cts", c_blocks, b_blocks, precision=HIGH)
    weighted = scores[..., None] * decay_map
    mixing = weighted * d_blocks[:, None, :, :]
    inside = jnp.einsum("ctsh,cshp->cthp", mixing, x_blocks, precision=HIGH)
    carried_raw = jnp.einsum("ctn,chpn->cthp", c_blocks, block_entry, precision=HIGH)
    start_decay = jnp.exp(cum_blocks)
    ssm_blocks = inside + start_decay[..., None] * carried_raw
    skip_rep = jnp.repeat(d_skip, head_dim)
    ssm_out = ssm_blocks.reshape(length, row_width) + skip_rep[None, :] * x_act
    z_float = z_proj.astype(jnp.float32)
    gate_act = jax.nn.silu(z_float)
    gated_out = ssm_out * gate_act
    grad_float = grad_out.astype(jnp.float32)
    scaled_grad = norm_gain[None, :] * grad_float
    norm_sums = all_sum(
        jnp.stack(
            [jnp.sum(gated_out * gated_out, axis=1), jnp.sum(scaled_grad * gated_out, axis=1)]
        ),
        "head",
    )
    square_sum, cross_sum = norm_sums[0], norm_sums[1]
    inv_rms = lax.rsqrt(square_sum / channels + EPS)[:, None]
    y_out = (gated_out * inv_rms * norm_gain[None, :]).astype(jnp.bfloat16)
    grad_gain_part = jnp.sum(grad_float * gated_out * inv_rms, axis=0)
    grad_gated = inv_rms * scaled_grad - gated_out * (inv_rms * inv_rms * inv_rms) * (
        cross_sum[:, None] / channels
    )
    grad_ssm = grad_gated * gate_act
    grad_z = (grad_gated * ssm_out * silu_grad(z_float)).astype(jnp.bfloat16)
    grad_skip_part = jnp.sum((grad_ssm * x_act).reshape(length, head_count, head_dim), axis=(0, 2))
    grad_blocks = grad_ssm.reshape(blocks, GROUP, head_count, head_dim)
    start_map = start_decay[..., None] * grad_blocks
    local_pull = jnp.einsum("cthp,ctn->chpn", start_map, c_blocks, precision=HIGH)
    shard_pull = jnp.sum(jnp.exp(prefix_log)[:, :, None, None] * local_pull, axis=0)

    leaving = exclusive_scan(shard_decay, shard_pull, "ctx", -1)
    running = leaving
    block_exit = [None] * blocks
    for index in reversed(range(blocks)):
        block_exit[index] = running
        running = block_decay[index][:, None, None] * running + local_pull[index]
    block_exit = jnp.stack(block_exit)

    b_exit = jnp.einsum("csn,chpn->cshp", b_blocks, block_exit, precision=HIGH)
    pulled = (
        jnp.einsum("ctsh,cthp->cshp", weighted, grad_blocks, precision=HIGH)
        + tail_decay[..., None] * b_exit
    )
    grad_x_blocks = d_blocks[..., None] * pulled
    grad_step_blocks = jnp.sum(x_blocks * pulled, axis=3)
    pair_grad = jnp.einsum("cthp,cshp->ctsh", grad_blocks, x_blocks, precision=HIGH)
    masked = pair_grad * decay_map * d_blocks[:, None, :, :]
    grad_scores = jnp.sum(masked, axis=3)
    grad_c_blocks = jnp.einsum("cts,csn->ctn", grad_scores, b_blocks, precision=HIGH)
    grad_b_blocks = jnp.einsum("cts,ctn->csn", grad_scores, c_blocks, precision=HIGH)
    through = masked * scores[..., None]
    grad_cum = jnp.sum(through, axis=2) - jnp.sum(through, axis=1)
    grad_cum = grad_cum + jnp.sum(start_map * carried_raw, axis=3)
    grad_c_blocks = grad_c_blocks + jnp.einsum(
        "cthp,chpn->ctn", start_map, block_entry, precision=HIGH
    )
    release = tail_weight * jnp.sum(x_blocks * b_exit, axis=3)
    grad_cum = grad_cum - release
    end_total = jnp.sum(release, axis=1) + jnp.exp(block_ends) * jnp.sum(
        block_entry * block_exit, axis=(2, 3)
    )
    grad_cum = jnp.concatenate(
        [grad_cum[:, :-1], grad_cum[:, -1:] + end_total[:, None, :]], axis=1
    )
    grad_log_blocks = jnp.flip(jnp.cumsum(jnp.flip(grad_cum, 1), axis=1), 1)
    grad_b_blocks = grad_b_blocks + jnp.einsum(
        "cshp,chpn->csn", tail_weight[..., None] * x_blocks, block_exit, precision=HIGH
    )

    grad_log_rows = grad_log_blocks.reshape(length, head_count)
    grad_step_rows = (
        grad_step_blocks.reshape(length, head_count) - decay_rate[None, :] * grad_log_rows
    )
    grad_alog_part = decay_rate * -jnp.sum(step_size * grad_log_rows, axis=0)
    grad_dt = (grad_step_rows * jax.nn.sigmoid(dt_raw).T).T
    grad_x_act = grad_x_blocks.reshape(length, row_width) + skip_rep[None, :] * grad_ssm
    grad_bc_act = jnp.concatenate(
        [grad_b_blocks.reshape(length, state_dim), grad_c_blocks.reshape(length, state_dim)], axis=1
    )
    grad_x_pre = grad_x_act * silu_grad(x_pre)
    grad_bc_pre = grad_bc_act * silu_grad(bc_pre)
    ahead = passed_along(
        jnp.concatenate([grad_x_pre[: tap_count - 1], grad_bc_pre[: tap_count - 1]], axis=1),
        "ctx",
        -1,
    )
    x_ahead = jnp.concatenate([grad_x_pre, ahead[:, :row_width]], axis=0)
    bc_ahead = jnp.concatenate([grad_bc_pre, ahead[:, row_width:]], axis=0)
    grad_x = back_taps(x_ahead, conv_x, length).astype(jnp.bfloat16)
    bc_back = back_taps(bc_ahead, conv_bc, length)
    shares = sum_scatter(bc_back, "head")
    grad_b = shares[:, :state_dim].astype(jnp.bfloat16)
    grad_c = shares[:, state_dim:].astype(jnp.bfloat16)
    grad_convx_part = weight_taps(grad_x_pre, x_padded, length, tap_count)
    grad_convbc_part = weight_taps(grad_bc_pre, bc_padded, length, tap_count)
    per_head = jnp.concatenate(
        [grad_alog_part, grad_skip_part, grad_convx_part.reshape(-1), grad_gain_part]
    )
    totals = all_sum(jnp.concatenate([per_head, grad_convbc_part.reshape(-1)]), "ctx")
    per_size = per_head.shape[0]
    grad_alog = totals[:head_count]
    grad_dskip = totals[head_count : 2 * head_count]
    convx_size = grad_convx_part.size
    grad_convx = totals[2 * head_count : 2 * head_count + convx_size].reshape(
        grad_convx_part.shape
    )
    grad_gain = totals[2 * head_count + convx_size : per_size]
    grad_convbc = all_sum(totals[per_size:], "head").reshape(grad_convbc_part.shape)
    return (
        y_out,
        grad_x,
        grad_z,
        grad_b,
        grad_c,
        grad_dt,
        grad_alog,
        grad_dskip,
        grad_convx,
        grad_convbc,
        grad_gain,
    )


def solution(mesh):
    return jax.shard_map(
        local,
        mesh=mesh,
        in_specs=(
            P("ctx", "head"),
            P("ctx", "head"),
            P("ctx", None),
            P("ctx", None),
            P("head", "ctx"),
            P("head"),
            P("head"),
            P(None, "head"),
            P(),
            P("head"),
            P("ctx", "head"),
        ),
        out_specs=(
            P("ctx", "head"),
            P("ctx", "head"),
            P("ctx", "head"),
            P(("ctx", "head"), None),
            P(("ctx", "head"), None),
            P("head", "ctx"),
            P("head"),
            P("head"),
            P(None, "head"),
            P(),
            P("head"),
        ),
        check_vma=False,
    )
```

```python
import jax
import jax.numpy as jnp
from jax import lax
from jax.sharding import PartitionSpec as P

HEADS = 128
HEAD_DIM = 64
GROUP = 256


HIGH = lax.Precision.HIGHEST
EPS = 1e-05


def passed_along(block, axis, distance):
    devices = range(lax.axis_size(axis))
    route = [(i - distance, i) for i in devices if i - distance in devices]
    return lax.ppermute(block, axis, route)


def exclusive_scan(decay, state, axis, direction):
    count = lax.axis_size(axis)
    rows = state.shape[1]

    def packed(decay_part, state_part):
        decay_row = jnp.broadcast_to(decay_part[:, None, None], state_part[:, :1].shape)
        return jnp.concatenate([state_part, decay_row], axis=1)

    def unpacked(part):
        return part[:, rows, 0], part[:, :rows]

    first = 0 if direction > 0 else 1
    second = 1 - first
    pairs = count // 2
    in_pair = [(2 * pair + first, 2 * pair + second) for pair in range(pairs)]
    front_decay, front_state = unpacked(lax.ppermute(packed(decay, state), axis, in_pair))
    inc_state = decay[:, None, None] * front_state + state
    inc_decay = decay * front_decay
    exc_decay = jnp.ones_like(decay)
    exc_state = jnp.zeros_like(state)
    distance = 1
    while distance < pairs:
        route = [
            (2 * pair + second, 2 * (pair + distance * direction) + second)
            for pair in range(pairs)
            if 0 <= pair + distance * direction < pairs
        ]
        got_decay, got_state = unpacked(
            lax.ppermute(packed(inc_decay, inc_state), axis, route)
        )
        exc_state = exc_state + exc_decay[:, None, None] * got_state
        exc_decay = exc_decay * got_decay
        if 2 * distance < pairs:
            inc_state = inc_state + inc_decay[:, None, None] * got_state
            inc_decay = inc_decay * got_decay
        distance *= 2
    back = lax.ppermute(exc_state, axis, [(target, source) for source, target in in_pair])
    is_second = lax.axis_index(axis) % 2 == second
    return jnp.where(is_second, front_decay[:, None, None] * exc_state + front_state, back)


def digit_plan(count):
    plan = []
    stride = 1
    while stride < count:
        radix = 4 if (count // stride) % 4 == 0 else 2
        plan.append((stride, radix))
        stride *= radix
    return plan


def shifted(block, axis, stride, radix, shift):
    route = []
    for source in range(lax.axis_size(axis)):
        digit = (source // stride) % radix
        route.append((source, source + ((digit + shift) % radix - digit) * stride))
    return lax.ppermute(block, axis, route)


def all_sum(block, axis):
    for stride, radix in digit_plan(lax.axis_size(axis)):
        got = [block] + [shifted(block, axis, stride, radix, shift) for shift in range(1, radix)]
        digit = (lax.axis_index(axis) // stride) % radix
        ordered = jnp.take(jnp.stack(got), (digit - jnp.arange(radix)) % radix, axis=0)
        block = ordered[0]
        for index in range(1, radix):
            block = block + ordered[index]
    return block


def sum_scatter(block, axis):
    count = lax.axis_size(axis)
    plan = digit_plan(count)
    trailing = block.ndim - 1
    chunk = block.shape[0] // count
    block = block.reshape(tuple(radix for _, radix in reversed(plan)) + (chunk,) + block.shape[1:])
    for stride, radix in plan:
        digit = (lax.axis_index(axis) // stride) % radix
        where = block.ndim - 2 - trailing
        total = lax.dynamic_index_in_dim(block, digit, axis=where, keepdims=False)
        for shift in range(1, radix):
            part = lax.dynamic_index_in_dim(block, (digit + shift) % radix, axis=where, keepdims=False)
            total = total + shifted(part, axis, stride, radix, shift)
        block = total
    return block


def silu_grad(value):
    sigma = jax.nn.sigmoid(value)
    return sigma * (1.0 + value * (1.0 - sigma))


def tap_sum(padded, weight, count):
    summed = jnp.zeros((count, padded.shape[1]), jnp.float32)
    for offset in range(weight.shape[0]):
        summed = summed + weight[offset][None, :] * padded[offset : offset + count].astype(
            jnp.float32
        )
    return summed


def back_taps(ahead, weight, count):
    final_tap = weight.shape[0] - 1
    summed = jnp.zeros((count, ahead.shape[1]), jnp.float32)
    for offset in range(weight.shape[0]):
        summed = (
            summed
            + weight[offset][None, :] * ahead[final_tap - offset : final_tap - offset + count]
        )
    return summed


def weight_taps(grad_pre, padded, count, tap_count):
    return jnp.stack(
        [
            jnp.sum(grad_pre * padded[offset : offset + count].astype(jnp.float32), axis=0)
            for offset in range(tap_count)
        ]
    )


def decay_table(cum_blocks):
    size_rows = cum_blocks.shape[1]
    row_ids = lax.broadcasted_iota(jnp.int32, (size_rows, size_rows), 0)
    col_ids = lax.broadcasted_iota(jnp.int32, (size_rows, size_rows), 1)
    allowed = (col_ids <= row_ids)[None, :, :, None]
    spread = cum_blocks[:, :, None, :] - cum_blocks[:, None, :, :]
    return jnp.where(allowed, jnp.exp(jnp.where(allowed, spread, 0.0)), 0.0)


def local(
    x_proj, z_proj, b_proj, c_proj, dt_raw, a_log, d_skip, conv_x, conv_bc, norm_gain, grad_out
):
    length = x_proj.shape[0]
    head_count = dt_raw.shape[0]
    row_width = x_proj.shape[1]
    head_dim = row_width // head_count
    state_dim = b_proj.shape[1]
    tap_count = conv_x.shape[0]
    blocks = length // GROUP
    channels = HEADS * HEAD_DIM
    bc_proj = jnp.concatenate([b_proj, c_proj], axis=1)
    edges = passed_along(
        jnp.concatenate(
            [x_proj[length - tap_count + 1 :], bc_proj[length - tap_count + 1 :]], axis=1
        ),
        "ctx",
        1,
    )
    x_padded = jnp.concatenate([edges[:, :row_width], x_proj], axis=0)
    bc_padded = jnp.concatenate([edges[:, row_width:], bc_proj], axis=0)
    x_pre = tap_sum(x_padded, conv_x, length)
    bc_pre = tap_sum(bc_padded, conv_bc, length)
    x_act = jax.nn.silu(x_pre)
    bc_act = jax.nn.silu(bc_pre)
    decay_rate = jnp.exp(a_log)
    step_size = jax.nn.softplus(dt_raw).T
    x_blocks = x_act.reshape(blocks, GROUP, head_count, head_dim)
    b_blocks = bc_act[:, :state_dim].reshape(blocks, GROUP, state_dim)
    c_blocks = bc_act[:, state_dim:].reshape(blocks, GROUP, state_dim)
    d_blocks = step_size.reshape(blocks, GROUP, head_count)
    cum_blocks = jnp.cumsum(
        (-step_size * decay_rate[None, :]).reshape(blocks, GROUP, head_count), axis=1
    )
    block_ends = cum_blocks[:, -1, :]
    block_decay = jnp.exp(block_ends)
    tail_decay = jnp.exp(cum_blocks[:, -1:, :] - cum_blocks)
    tail_weight = tail_decay * d_blocks
    block_states = jnp.einsum(
        "cshp,csn->chpn", tail_weight[..., None] * x_blocks, b_blocks, precision=HIGH
    )

    running = jnp.zeros((head_count, head_dim, state_dim), jnp.float32)
    local_entering = []
    for index in range(blocks):
        local_entering.append(running)
        running = block_decay[index][:, None, None] * running + block_states[index]
    shard_state = running
    local_entering = jnp.stack(local_entering)
    prefix_log = jnp.cumsum(block_ends, axis=0) - block_ends
    shard_decay = jnp.exp(jnp.sum(block_ends, axis=0))

    entering = exclusive_scan(shard_decay, shard_state, "ctx", 1)
    block_entry = jnp.exp(prefix_log)[:, :, None, None] * entering[None] + local_entering

    decay_map = decay_table(cum_blocks)
    scores = jnp.einsum("ctn,csn->cts", c_blocks, b_blocks, precision=HIGH)
    weighted = scores[..., None] * decay_map
    mixing = weighted * d_blocks[:, None, :, :]
    inside = jnp.einsum("ctsh,cshp->cthp", mixing, x_blocks, precision=HIGH)
    carried_raw = jnp.einsum("ctn,chpn->cthp", c_blocks, block_entry, precision=HIGH)
    start_decay = jnp.exp(cum_blocks)
    ssm_blocks = inside + start_decay[..., None] * carried_raw
    skip_rep = jnp.repeat(d_skip, head_dim)
    ssm_out = ssm_blocks.reshape(length, row_width) + skip_rep[None, :] * x_act
    z_float = z_proj.astype(jnp.float32)
    gate_act = jax.nn.silu(z_float)
    gated_out = ssm_out * gate_act
    grad_float = grad_out.astype(jnp.float32)
    scaled_grad = norm_gain[None, :] * grad_float
    norm_sums = all_sum(
        jnp.stack(
            [jnp.sum(gated_out * gated_out, axis=1), jnp.sum(scaled_grad * gated_out, axis=1)]
        ),
        "head",
    )
    square_sum, cross_sum = norm_sums[0], norm_sums[1]
    inv_rms = lax.rsqrt(square_sum / channels + EPS)[:, None]
    y_out = (gated_out * inv_rms * norm_gain[None, :]).astype(jnp.bfloat16)
    grad_gain_part = jnp.sum(grad_float * gated_out * inv_rms, axis=0)
    grad_gated = inv_rms * scaled_grad - gated_out * (inv_rms * inv_rms * inv_rms) * (
        cross_sum[:, None] / channels
    )
    grad_ssm = grad_gated * gate_act
    grad_z = (grad_gated * ssm_out * silu_grad(z_float)).astype(jnp.bfloat16)
    grad_skip_part = jnp.sum((grad_ssm * x_act).reshape(length, head_count, head_dim), axis=(0, 2))
    grad_blocks = grad_ssm.reshape(blocks, GROUP, head_count, head_dim)
    start_map = start_decay[..., None] * grad_blocks
    local_pull = jnp.einsum("cthp,ctn->chpn", start_map, c_blocks, precision=HIGH)
    shard_pull = jnp.sum(jnp.exp(prefix_log)[:, :, None, None] * local_pull, axis=0)

    leaving = exclusive_scan(shard_decay, shard_pull, "ctx", -1)
    running = leaving
    block_exit = [None] * blocks
    for index in reversed(range(blocks)):
        block_exit[index] = running
        running = block_decay[index][:, None, None] * running + local_pull[index]
    block_exit = jnp.stack(block_exit)

    b_exit = jnp.einsum("csn,chpn->cshp", b_blocks, block_exit, precision=HIGH)
    pulled = (
        jnp.einsum("ctsh,cthp->cshp", weighted, grad_blocks, precision=HIGH)
        + tail_decay[..., None] * b_exit
    )
    grad_x_blocks = d_blocks[..., None] * pulled
    grad_step_blocks = jnp.sum(x_blocks * pulled, axis=3)
    pair_grad = jnp.einsum("cthp,cshp->ctsh", grad_blocks, x_blocks, precision=HIGH)
    masked = pair_grad * decay_map * d_blocks[:, None, :, :]
    grad_scores = jnp.sum(masked, axis=3)
    grad_c_blocks = jnp.einsum("cts,csn->ctn", grad_scores, b_blocks, precision=HIGH)
    grad_b_blocks = jnp.einsum("cts,ctn->csn", grad_scores, c_blocks, precision=HIGH)
    through = masked * scores[..., None]
    grad_cum = jnp.sum(through, axis=2) - jnp.sum(through, axis=1)
    grad_cum = grad_cum + jnp.sum(start_map * carried_raw, axis=3)
    grad_c_blocks = grad_c_blocks + jnp.einsum(
        "cthp,chpn->ctn", start_map, block_entry, precision=HIGH
    )
    release = tail_weight * jnp.sum(x_blocks * b_exit, axis=3)
    grad_cum = grad_cum - release
    end_total = jnp.sum(release, axis=1) + jnp.exp(block_ends) * jnp.sum(
        block_entry * block_exit, axis=(2, 3)
    )
    grad_cum = jnp.concatenate(
        [grad_cum[:, :-1], grad_cum[:, -1:] + end_total[:, None, :]], axis=1
    )
    grad_log_blocks = jnp.flip(jnp.cumsum(jnp.flip(grad_cum, 1), axis=1), 1)
    grad_b_blocks = grad_b_blocks + jnp.einsum(
        "cshp,chpn->csn", tail_weight[..., None] * x_blocks, block_exit, precision=HIGH
    )

    grad_log_rows = grad_log_blocks.reshape(length, head_count)
    grad_step_rows = (
        grad_step_blocks.reshape(length, head_count) - decay_rate[None, :] * grad_log_rows
    )
    grad_alog_part = decay_rate * -jnp.sum(step_size * grad_log_rows, axis=0)
    grad_dt = (grad_step_rows * jax.nn.sigmoid(dt_raw).T).T
    grad_x_act = grad_x_blocks.reshape(length, row_width) + skip_rep[None, :] * grad_ssm
    grad_bc_act = jnp.concatenate(
        [grad_b_blocks.reshape(length, state_dim), grad_c_blocks.reshape(length, state_dim)], axis=1
    )
    grad_x_pre = grad_x_act * silu_grad(x_pre)
    grad_bc_pre = grad_bc_act * silu_grad(bc_pre)
    ahead = passed_along(
        jnp.concatenate([grad_x_pre[: tap_count - 1], grad_bc_pre[: tap_count - 1]], axis=1),
        "ctx",
        -1,
    )
    x_ahead = jnp.concatenate([grad_x_pre, ahead[:, :row_width]], axis=0)
    bc_ahead = jnp.concatenate([grad_bc_pre, ahead[:, row_width:]], axis=0)
    grad_x = back_taps(x_ahead, conv_x, length).astype(jnp.bfloat16)
    bc_back = back_taps(bc_ahead, conv_bc, length)
    shares = sum_scatter(bc_back, "head")
    grad_b = shares[:, :state_dim].astype(jnp.bfloat16)
    grad_c = shares[:, state_dim:].astype(jnp.bfloat16)
    grad_convx_part = weight_taps(grad_x_pre, x_padded, length, tap_count)
    grad_convbc_part = weight_taps(grad_bc_pre, bc_padded, length, tap_count)
    per_head = jnp.concatenate(
        [grad_alog_part, grad_skip_part, grad_convx_part.reshape(-1), grad_gain_part]
    )
    totals = all_sum(jnp.concatenate([per_head, grad_convbc_part.reshape(-1)]), "ctx")
    per_size = per_head.shape[0]
    grad_alog = totals[:head_count]
    grad_dskip = totals[head_count : 2 * head_count]
    convx_size = grad_convx_part.size
    grad_convx = totals[2 * head_count : 2 * head_count + convx_size].reshape(
        grad_convx_part.shape
    )
    grad_gain = totals[2 * head_count + convx_size : per_size]
    grad_convbc = all_sum(totals[per_size:], "head").reshape(grad_convbc_part.shape)
    return (
        y_out,
        grad_x,
        grad_z,
        grad_b,
        grad_c,
        grad_dt,
        grad_alog,
        grad_dskip,
        grad_convx,
        grad_convbc,
        grad_gain,
    )


def solution(mesh):
    return jax.shard_map(
        local,
        mesh=mesh,
        in_specs=(
            P("ctx", "head"),
            P("ctx", "head"),
            P("ctx", None),
            P("ctx", None),
            P("head", "ctx"),
            P("head"),
            P("head"),
            P(None, "head"),
            P(),
            P("head"),
            P("ctx", "head"),
        ),
        out_specs=(
            P("ctx", "head"),
            P("ctx", "head"),
            P("ctx", "head"),
            P(("ctx", "head"), None),
            P(("ctx", "head"), None),
            P("head", "ctx"),
            P("head"),
            P("head"),
            P(None, "head"),
            P(),
            P("head"),
        ),
        check_vma=False,
    )
```

```python
import jax
import jax.numpy as jnp
from jax import lax
from jax.sharding import PartitionSpec as P

HEADS = 128
HEAD_DIM = 64
GROUP = 256


HIGH = lax.Precision.HIGHEST
EPS = 1e-05


def passed_along(block, axis, distance):
    devices = range(lax.axis_size(axis))
    route = [(i - distance, i) for i in devices if i - distance in devices]
    return lax.ppermute(block, axis, route)


def exclusive_scan(decay, state, axis, direction):
    count = lax.axis_size(axis)
    rows = state.shape[1]

    def packed(decay_part, state_part):
        decay_row = jnp.broadcast_to(decay_part[:, None, None], state_part[:, :1].shape)
        return jnp.concatenate([state_part, decay_row], axis=1)

    def unpacked(part):
        return part[:, rows, 0], part[:, :rows]

    first = 0 if direction > 0 else 1
    second = 1 - first
    pairs = count // 2
    in_pair = [(2 * pair + first, 2 * pair + second) for pair in range(pairs)]
    front_decay, front_state = unpacked(lax.ppermute(packed(decay, state), axis, in_pair))
    inc_state = decay[:, None, None] * front_state + state
    inc_decay = decay * front_decay
    exc_decay = jnp.ones_like(decay)
    exc_state = jnp.zeros_like(state)
    distance = 1
    while distance < pairs:
        route = [
            (2 * pair + second, 2 * (pair + distance * direction) + second)
            for pair in range(pairs)
            if 0 <= pair + distance * direction < pairs
        ]
        got_decay, got_state = unpacked(
            lax.ppermute(packed(inc_decay, inc_state), axis, route)
        )
        exc_state = exc_state + exc_decay[:, None, None] * got_state
        exc_decay = exc_decay * got_decay
        if 2 * distance < pairs:
            inc_state = inc_state + inc_decay[:, None, None] * got_state
            inc_decay = inc_decay * got_decay
        distance *= 2
    back = lax.ppermute(exc_state, axis, [(target, source) for source, target in in_pair])
    is_second = lax.axis_index(axis) % 2 == second
    return jnp.where(is_second, front_decay[:, None, None] * exc_state + front_state, back)


def digit_plan(count):
    plan = []
    stride = 1
    while stride < count:
        radix = 4 if (count // stride) % 4 == 0 else 2
        plan.append((stride, radix))
        stride *= radix
    return plan


def shifted(block, axis, stride, radix, shift):
    route = []
    for source in range(lax.axis_size(axis)):
        digit = (source // stride) % radix
        route.append((source, source + ((digit + shift) % radix - digit) * stride))
    return lax.ppermute(block, axis, route)


def all_sum(block, axis):
    for stride, radix in digit_plan(lax.axis_size(axis)):
        got = [block] + [shifted(block, axis, stride, radix, shift) for shift in range(1, radix)]
        digit = (lax.axis_index(axis) // stride) % radix
        ordered = jnp.take(jnp.stack(got), (digit - jnp.arange(radix)) % radix, axis=0)
        block = ordered[0]
        for index in range(1, radix):
            block = block + ordered[index]
    return block


def sum_scatter(block, extra, axis):
    count = lax.axis_size(axis)
    plan = digit_plan(count)
    trailing = block.ndim - 1
    chunk = block.shape[0] // count
    block = block.reshape(tuple(radix for _, radix in reversed(plan)) + (chunk,) + block.shape[1:])
    for stride, radix in plan:
        digit = (lax.axis_index(axis) // stride) % radix
        where = block.ndim - 2 - trailing
        total = lax.dynamic_index_in_dim(block, digit, axis=where, keepdims=False)
        size = total.size
        extras = [extra]
        for shift in range(1, radix):
            part = lax.dynamic_index_in_dim(block, (digit + shift) % radix, axis=where, keepdims=False)
            got = shifted(jnp.concatenate([part.reshape(-1), extra]), axis, stride, radix, shift)
            total = total + got[:size].reshape(total.shape)
            extras.append(got[size:])
        ordered = jnp.take(jnp.stack(extras), (digit - jnp.arange(radix)) % radix, axis=0)
        extra = ordered[0]
        for index in range(1, radix):
            extra = extra + ordered[index]
        block = total
    return block, extra


def silu_grad(value):
    sigma = jax.nn.sigmoid(value)
    return sigma * (1.0 + value * (1.0 - sigma))


def tap_sum(padded, weight, count):
    summed = jnp.zeros((count, padded.shape[1]), jnp.float32)
    for offset in range(weight.shape[0]):
        summed = summed + weight[offset][None, :] * padded[offset : offset + count].astype(
            jnp.float32
        )
    return summed


def back_taps(ahead, weight, count):
    final_tap = weight.shape[0] - 1
    summed = jnp.zeros((count, ahead.shape[1]), jnp.float32)
    for offset in range(weight.shape[0]):
        summed = (
            summed
            + weight[offset][None, :] * ahead[final_tap - offset : final_tap - offset + count]
        )
    return summed


def weight_taps(grad_pre, padded, count, tap_count):
    return jnp.stack(
        [
            jnp.sum(grad_pre * padded[offset : offset + count].astype(jnp.float32), axis=0)
            for offset in range(tap_count)
        ]
    )


def decay_table(cum_blocks):
    size_rows = cum_blocks.shape[1]
    row_ids = lax.broadcasted_iota(jnp.int32, (size_rows, size_rows), 0)
    col_ids = lax.broadcasted_iota(jnp.int32, (size_rows, size_rows), 1)
    allowed = (col_ids <= row_ids)[None, :, :, None]
    spread = cum_blocks[:, :, None, :] - cum_blocks[:, None, :, :]
    return jnp.where(allowed, jnp.exp(jnp.where(allowed, spread, 0.0)), 0.0)


def local(
    x_proj, z_proj, b_proj, c_proj, dt_raw, a_log, d_skip, conv_x, conv_bc, norm_gain, grad_out
):
    length = x_proj.shape[0]
    head_count = dt_raw.shape[0]
    row_width = x_proj.shape[1]
    head_dim = row_width // head_count
    state_dim = b_proj.shape[1]
    tap_count = conv_x.shape[0]
    blocks = length // GROUP
    channels = HEADS * HEAD_DIM
    bc_proj = jnp.concatenate([b_proj, c_proj], axis=1)
    edges = passed_along(
        jnp.concatenate(
            [x_proj[length - tap_count + 1 :], bc_proj[length - tap_count + 1 :]], axis=1
        ),
        "ctx",
        1,
    )
    x_padded = jnp.concatenate([edges[:, :row_width], x_proj], axis=0)
    bc_padded = jnp.concatenate([edges[:, row_width:], bc_proj], axis=0)
    x_pre = tap_sum(x_padded, conv_x, length)
    bc_pre = tap_sum(bc_padded, conv_bc, length)
    x_act = jax.nn.silu(x_pre)
    bc_act = jax.nn.silu(bc_pre)
    decay_rate = jnp.exp(a_log)
    step_size = jax.nn.softplus(dt_raw).T
    x_blocks = x_act.reshape(blocks, GROUP, head_count, head_dim)
    b_blocks = bc_act[:, :state_dim].reshape(blocks, GROUP, state_dim)
    c_blocks = bc_act[:, state_dim:].reshape(blocks, GROUP, state_dim)
    d_blocks = step_size.reshape(blocks, GROUP, head_count)
    cum_blocks = jnp.cumsum(
        (-step_size * decay_rate[None, :]).reshape(blocks, GROUP, head_count), axis=1
    )
    block_ends = cum_blocks[:, -1, :]
    block_decay = jnp.exp(block_ends)
    tail_decay = jnp.exp(cum_blocks[:, -1:, :] - cum_blocks)
    tail_weight = tail_decay * d_blocks
    block_states = jnp.einsum(
        "cshp,csn->chpn", tail_weight[..., None] * x_blocks, b_blocks, precision=HIGH
    )

    running = jnp.zeros((head_count, head_dim, state_dim), jnp.float32)
    local_entering = []
    for index in range(blocks):
        local_entering.append(running)
        running = block_decay[index][:, None, None] * running + block_states[index]
    shard_state = running
    local_entering = jnp.stack(local_entering)
    prefix_log = jnp.cumsum(block_ends, axis=0) - block_ends
    shard_decay = jnp.exp(jnp.sum(block_ends, axis=0))

    entering = exclusive_scan(shard_decay, shard_state, "ctx", 1)
    block_entry = jnp.exp(prefix_log)[:, :, None, None] * entering[None] + local_entering

    decay_map = decay_table(cum_blocks)
    scores = jnp.einsum("ctn,csn->cts", c_blocks, b_blocks, precision=HIGH)
    weighted = scores[..., None] * decay_map
    mixing = weighted * d_blocks[:, None, :, :]
    inside = jnp.einsum("ctsh,cshp->cthp", mixing, x_blocks, precision=HIGH)
    carried_raw = jnp.einsum("ctn,chpn->cthp", c_blocks, block_entry, precision=HIGH)
    start_decay = jnp.exp(cum_blocks)
    ssm_blocks = inside + start_decay[..., None] * carried_raw
    skip_rep = jnp.repeat(d_skip, head_dim)
    ssm_out = ssm_blocks.reshape(length, row_width) + skip_rep[None, :] * x_act
    z_float = z_proj.astype(jnp.float32)
    gate_act = jax.nn.silu(z_float)
    gated_out = ssm_out * gate_act
    grad_float = grad_out.astype(jnp.float32)
    scaled_grad = norm_gain[None, :] * grad_float
    norm_sums = all_sum(
        jnp.stack(
            [jnp.sum(gated_out * gated_out, axis=1), jnp.sum(scaled_grad * gated_out, axis=1)]
        ),
        "head",
    )
    square_sum, cross_sum = norm_sums[0], norm_sums[1]
    inv_rms = lax.rsqrt(square_sum / channels + EPS)[:, None]
    y_out = (gated_out * inv_rms * norm_gain[None, :]).astype(jnp.bfloat16)
    grad_gain_part = jnp.sum(grad_float * gated_out * inv_rms, axis=0)
    grad_gated = inv_rms * scaled_grad - gated_out * (inv_rms * inv_rms * inv_rms) * (
        cross_sum[:, None] / channels
    )
    grad_ssm = grad_gated * gate_act
    grad_z = (grad_gated * ssm_out * silu_grad(z_float)).astype(jnp.bfloat16)
    grad_skip_part = jnp.sum((grad_ssm * x_act).reshape(length, head_count, head_dim), axis=(0, 2))
    grad_blocks = grad_ssm.reshape(blocks, GROUP, head_count, head_dim)
    start_map = start_decay[..., None] * grad_blocks
    local_pull = jnp.einsum("cthp,ctn->chpn", start_map, c_blocks, precision=HIGH)
    shard_pull = jnp.sum(jnp.exp(prefix_log)[:, :, None, None] * local_pull, axis=0)

    leaving = exclusive_scan(shard_decay, shard_pull, "ctx", -1)
    running = leaving
    block_exit = [None] * blocks
    for index in reversed(range(blocks)):
        block_exit[index] = running
        running = block_decay[index][:, None, None] * running + local_pull[index]
    block_exit = jnp.stack(block_exit)

    b_exit = jnp.einsum("csn,chpn->cshp", b_blocks, block_exit, precision=HIGH)
    pulled = (
        jnp.einsum("ctsh,cthp->cshp", weighted, grad_blocks, precision=HIGH)
        + tail_decay[..., None] * b_exit
    )
    grad_x_blocks = d_blocks[..., None] * pulled
    grad_step_blocks = jnp.sum(x_blocks * pulled, axis=3)
    pair_grad = jnp.einsum("cthp,cshp->ctsh", grad_blocks, x_blocks, precision=HIGH)
    masked = pair_grad * decay_map * d_blocks[:, None, :, :]
    grad_scores = jnp.sum(masked, axis=3)
    grad_c_blocks = jnp.einsum("cts,csn->ctn", grad_scores, b_blocks, precision=HIGH)
    grad_b_blocks = jnp.einsum("cts,ctn->csn", grad_scores, c_blocks, precision=HIGH)
    through = masked * scores[..., None]
    grad_cum = jnp.sum(through, axis=2) - jnp.sum(through, axis=1)
    grad_cum = grad_cum + jnp.sum(start_map * carried_raw, axis=3)
    grad_c_blocks = grad_c_blocks + jnp.einsum(
        "cthp,chpn->ctn", start_map, block_entry, precision=HIGH
    )
    release = tail_weight * jnp.sum(x_blocks * b_exit, axis=3)
    grad_cum = grad_cum - release
    end_total = jnp.sum(release, axis=1) + jnp.exp(block_ends) * jnp.sum(
        block_entry * block_exit, axis=(2, 3)
    )
    grad_cum = jnp.concatenate(
        [grad_cum[:, :-1], grad_cum[:, -1:] + end_total[:, None, :]], axis=1
    )
    grad_log_blocks = jnp.flip(jnp.cumsum(jnp.flip(grad_cum, 1), axis=1), 1)
    grad_b_blocks = grad_b_blocks + jnp.einsum(
        "cshp,chpn->csn", tail_weight[..., None] * x_blocks, block_exit, precision=HIGH
    )

    grad_log_rows = grad_log_blocks.reshape(length, head_count)
    grad_step_rows = (
        grad_step_blocks.reshape(length, head_count) - decay_rate[None, :] * grad_log_rows
    )
    grad_alog_part = decay_rate * -jnp.sum(step_size * grad_log_rows, axis=0)
    grad_dt = (grad_step_rows * jax.nn.sigmoid(dt_raw).T).T
    grad_x_act = grad_x_blocks.reshape(length, row_width) + skip_rep[None, :] * grad_ssm
    grad_bc_act = jnp.concatenate(
        [grad_b_blocks.reshape(length, state_dim), grad_c_blocks.reshape(length, state_dim)], axis=1
    )
    grad_x_pre = grad_x_act * silu_grad(x_pre)
    grad_bc_pre = grad_bc_act * silu_grad(bc_pre)
    ahead = passed_along(
        jnp.concatenate([grad_x_pre[: tap_count - 1], grad_bc_pre[: tap_count - 1]], axis=1),
        "ctx",
        -1,
    )
    x_ahead = jnp.concatenate([grad_x_pre, ahead[:, :row_width]], axis=0)
    bc_ahead = jnp.concatenate([grad_bc_pre, ahead[:, row_width:]], axis=0)
    grad_x = back_taps(x_ahead, conv_x, length).astype(jnp.bfloat16)
    bc_back = back_taps(bc_ahead, conv_bc, length)
    grad_convx_part = weight_taps(grad_x_pre, x_padded, length, tap_count)
    grad_convbc_part = weight_taps(grad_bc_pre, bc_padded, length, tap_count)
    per_head = jnp.concatenate(
        [grad_alog_part, grad_skip_part, grad_convx_part.reshape(-1), grad_gain_part]
    )
    totals = all_sum(jnp.concatenate([per_head, grad_convbc_part.reshape(-1)]), "ctx")
    per_size = per_head.shape[0]
    shares, convbc_total = sum_scatter(bc_back, totals[per_size:], "head")
    grad_b = shares[:, :state_dim].astype(jnp.bfloat16)
    grad_c = shares[:, state_dim:].astype(jnp.bfloat16)
    grad_alog = totals[:head_count]
    grad_dskip = totals[head_count : 2 * head_count]
    convx_size = grad_convx_part.size
    grad_convx = totals[2 * head_count : 2 * head_count + convx_size].reshape(
        grad_convx_part.shape
    )
    grad_gain = totals[2 * head_count + convx_size : per_size]
    grad_convbc = convbc_total.reshape(grad_convbc_part.shape)
    return (
        y_out,
        grad_x,
        grad_z,
        grad_b,
        grad_c,
        grad_dt,
        grad_alog,
        grad_dskip,
        grad_convx,
        grad_convbc,
        grad_gain,
    )


def solution(mesh):
    return jax.shard_map(
        local,
        mesh=mesh,
        in_specs=(
            P("ctx", "head"),
            P("ctx", "head"),
            P("ctx", None),
            P("ctx", None),
            P("head", "ctx"),
            P("head"),
            P("head"),
            P(None, "head"),
            P(),
            P("head"),
            P("ctx", "head"),
        ),
        out_specs=(
            P("ctx", "head"),
            P("ctx", "head"),
            P("ctx", "head"),
            P(("ctx", "head"), None),
            P(("ctx", "head"), None),
            P("head", "ctx"),
            P("head"),
            P("head"),
            P(None, "head"),
            P(),
            P("head"),
        ),
        check_vma=False,
    )
```

```python
import jax
import jax.numpy as jnp
from jax import lax
from jax.sharding import PartitionSpec as P

HEADS = 128
HEAD_DIM = 64
GROUP = 256


HIGH = lax.Precision.HIGHEST
EPS = 1e-05


def passed_along(block, axis, distance):
    devices = range(lax.axis_size(axis))
    route = [(i - distance, i) for i in devices if i - distance in devices]
    return lax.ppermute(block, axis, route)


def exclusive_scan(decay, state, axis, direction):
    count = lax.axis_size(axis)
    rows = state.shape[1]

    def packed(decay_part, state_part):
        decay_row = jnp.broadcast_to(decay_part[:, None, None], state_part[:, :1].shape)
        return jnp.concatenate([state_part, decay_row], axis=1)

    def unpacked(part):
        return part[:, rows, 0], part[:, :rows]

    first = 0 if direction > 0 else 1
    second = 1 - first
    pairs = count // 2
    in_pair = [(2 * pair + first, 2 * pair + second) for pair in range(pairs)]
    front_decay, front_state = unpacked(lax.ppermute(packed(decay, state), axis, in_pair))
    inc_state = decay[:, None, None] * front_state + state
    inc_decay = decay * front_decay
    exc_decay = jnp.ones_like(decay)
    exc_state = jnp.zeros_like(state)
    distance = 1
    while distance < pairs:
        route = [
            (2 * pair + second, 2 * (pair + distance * direction) + second)
            for pair in range(pairs)
            if 0 <= pair + distance * direction < pairs
        ]
        got_decay, got_state = unpacked(
            lax.ppermute(packed(inc_decay, inc_state), axis, route)
        )
        exc_state = exc_state + exc_decay[:, None, None] * got_state
        exc_decay = exc_decay * got_decay
        if 2 * distance < pairs:
            inc_state = inc_state + inc_decay[:, None, None] * got_state
            inc_decay = inc_decay * got_decay
        distance *= 2
    back = lax.ppermute(exc_state, axis, [(target, source) for source, target in in_pair])
    is_second = lax.axis_index(axis) % 2 == second
    return jnp.where(is_second, front_decay[:, None, None] * exc_state + front_state, back)


def digit_plan(count):
    plan = []
    stride = 1
    while stride < count:
        radix = 4 if (count // stride) % 4 == 0 else 2
        plan.append((stride, radix))
        stride *= radix
    return plan


def shifted(block, axis, stride, radix, shift):
    route = []
    for source in range(lax.axis_size(axis)):
        digit = (source // stride) % radix
        route.append((source, source + ((digit + shift) % radix - digit) * stride))
    return lax.ppermute(block, axis, route)


def all_sum(block, axis, one_round=False):
    plan = [(1, lax.axis_size(axis))] if one_round else digit_plan(lax.axis_size(axis))
    for stride, radix in plan:
        got = [block] + [shifted(block, axis, stride, radix, shift) for shift in range(1, radix)]
        digit = (lax.axis_index(axis) // stride) % radix
        ordered = jnp.take(jnp.stack(got), (digit - jnp.arange(radix)) % radix, axis=0)
        block = ordered[0]
        for index in range(1, radix):
            block = block + ordered[index]
    return block


def sum_scatter(block, extra, axis):
    count = lax.axis_size(axis)
    plan = digit_plan(count)
    trailing = block.ndim - 1
    chunk = block.shape[0] // count
    block = block.reshape(tuple(radix for _, radix in reversed(plan)) + (chunk,) + block.shape[1:])
    for stride, radix in plan:
        digit = (lax.axis_index(axis) // stride) % radix
        where = block.ndim - 2 - trailing
        total = lax.dynamic_index_in_dim(block, digit, axis=where, keepdims=False)
        size = total.size
        extras = [extra]
        for shift in range(1, radix):
            part = lax.dynamic_index_in_dim(block, (digit + shift) % radix, axis=where, keepdims=False)
            got = shifted(jnp.concatenate([part.reshape(-1), extra]), axis, stride, radix, shift)
            total = total + got[:size].reshape(total.shape)
            extras.append(got[size:])
        ordered = jnp.take(jnp.stack(extras), (digit - jnp.arange(radix)) % radix, axis=0)
        extra = ordered[0]
        for index in range(1, radix):
            extra = extra + ordered[index]
        block = total
    return block, extra


def silu_grad(value):
    sigma = jax.nn.sigmoid(value)
    return sigma * (1.0 + value * (1.0 - sigma))


def tap_sum(padded, weight, count):
    summed = jnp.zeros((count, padded.shape[1]), jnp.float32)
    for offset in range(weight.shape[0]):
        summed = summed + weight[offset][None, :] * padded[offset : offset + count].astype(
            jnp.float32
        )
    return summed


def back_taps(ahead, weight, count):
    final_tap = weight.shape[0] - 1
    summed = jnp.zeros((count, ahead.shape[1]), jnp.float32)
    for offset in range(weight.shape[0]):
        summed = (
            summed
            + weight[offset][None, :] * ahead[final_tap - offset : final_tap - offset + count]
        )
    return summed


def weight_taps(grad_pre, padded, count, tap_count):
    return jnp.stack(
        [
            jnp.sum(grad_pre * padded[offset : offset + count].astype(jnp.float32), axis=0)
            for offset in range(tap_count)
        ]
    )


def decay_table(cum_blocks):
    size_rows = cum_blocks.shape[1]
    row_ids = lax.broadcasted_iota(jnp.int32, (size_rows, size_rows), 0)
    col_ids = lax.broadcasted_iota(jnp.int32, (size_rows, size_rows), 1)
    allowed = (col_ids <= row_ids)[None, :, :, None]
    spread = cum_blocks[:, :, None, :] - cum_blocks[:, None, :, :]
    return jnp.where(allowed, jnp.exp(jnp.where(allowed, spread, 0.0)), 0.0)


def local(
    x_proj, z_proj, b_proj, c_proj, dt_raw, a_log, d_skip, conv_x, conv_bc, norm_gain, grad_out
):
    length = x_proj.shape[0]
    head_count = dt_raw.shape[0]
    row_width = x_proj.shape[1]
    head_dim = row_width // head_count
    state_dim = b_proj.shape[1]
    tap_count = conv_x.shape[0]
    blocks = length // GROUP
    channels = HEADS * HEAD_DIM
    bc_proj = jnp.concatenate([b_proj, c_proj], axis=1)
    edges = passed_along(
        jnp.concatenate(
            [x_proj[length - tap_count + 1 :], bc_proj[length - tap_count + 1 :]], axis=1
        ),
        "ctx",
        1,
    )
    x_padded = jnp.concatenate([edges[:, :row_width], x_proj], axis=0)
    bc_padded = jnp.concatenate([edges[:, row_width:], bc_proj], axis=0)
    x_pre = tap_sum(x_padded, conv_x, length)
    bc_pre = tap_sum(bc_padded, conv_bc, length)
    x_act = jax.nn.silu(x_pre)
    bc_act = jax.nn.silu(bc_pre)
    decay_rate = jnp.exp(a_log)
    step_size = jax.nn.softplus(dt_raw).T
    x_blocks = x_act.reshape(blocks, GROUP, head_count, head_dim)
    b_blocks = bc_act[:, :state_dim].reshape(blocks, GROUP, state_dim)
    c_blocks = bc_act[:, state_dim:].reshape(blocks, GROUP, state_dim)
    d_blocks = step_size.reshape(blocks, GROUP, head_count)
    cum_blocks = jnp.cumsum(
        (-step_size * decay_rate[None, :]).reshape(blocks, GROUP, head_count), axis=1
    )
    block_ends = cum_blocks[:, -1, :]
    block_decay = jnp.exp(block_ends)
    tail_decay = jnp.exp(cum_blocks[:, -1:, :] - cum_blocks)
    tail_weight = tail_decay * d_blocks
    block_states = jnp.einsum(
        "cshp,csn->chpn", tail_weight[..., None] * x_blocks, b_blocks, precision=HIGH
    )

    running = jnp.zeros((head_count, head_dim, state_dim), jnp.float32)
    local_entering = []
    for index in range(blocks):
        local_entering.append(running)
        running = block_decay[index][:, None, None] * running + block_states[index]
    shard_state = running
    local_entering = jnp.stack(local_entering)
    prefix_log = jnp.cumsum(block_ends, axis=0) - block_ends
    shard_decay = jnp.exp(jnp.sum(block_ends, axis=0))

    entering = exclusive_scan(shard_decay, shard_state, "ctx", 1)
    block_entry = jnp.exp(prefix_log)[:, :, None, None] * entering[None] + local_entering

    decay_map = decay_table(cum_blocks)
    scores = jnp.einsum("ctn,csn->cts", c_blocks, b_blocks, precision=HIGH)
    weighted = scores[..., None] * decay_map
    mixing = weighted * d_blocks[:, None, :, :]
    inside = jnp.einsum("ctsh,cshp->cthp", mixing, x_blocks, precision=HIGH)
    carried_raw = jnp.einsum("ctn,chpn->cthp", c_blocks, block_entry, precision=HIGH)
    start_decay = jnp.exp(cum_blocks)
    ssm_blocks = inside + start_decay[..., None] * carried_raw
    skip_rep = jnp.repeat(d_skip, head_dim)
    ssm_out = ssm_blocks.reshape(length, row_width) + skip_rep[None, :] * x_act
    z_float = z_proj.astype(jnp.float32)
    gate_act = jax.nn.silu(z_float)
    gated_out = ssm_out * gate_act
    grad_float = grad_out.astype(jnp.float32)
    scaled_grad = norm_gain[None, :] * grad_float
    norm_sums = all_sum(
        jnp.stack(
            [jnp.sum(gated_out * gated_out, axis=1), jnp.sum(scaled_grad * gated_out, axis=1)]
        ),
        "head",
        one_round=True,
    )
    square_sum, cross_sum = norm_sums[0], norm_sums[1]
    inv_rms = lax.rsqrt(square_sum / channels + EPS)[:, None]
    y_out = (gated_out * inv_rms * norm_gain[None, :]).astype(jnp.bfloat16)
    grad_gain_part = jnp.sum(grad_float * gated_out * inv_rms, axis=0)
    grad_gated = inv_rms * scaled_grad - gated_out * (inv_rms * inv_rms * inv_rms) * (
        cross_sum[:, None] / channels
    )
    grad_ssm = grad_gated * gate_act
    grad_z = (grad_gated * ssm_out * silu_grad(z_float)).astype(jnp.bfloat16)
    grad_skip_part = jnp.sum((grad_ssm * x_act).reshape(length, head_count, head_dim), axis=(0, 2))
    grad_blocks = grad_ssm.reshape(blocks, GROUP, head_count, head_dim)
    start_map = start_decay[..., None] * grad_blocks
    local_pull = jnp.einsum("cthp,ctn->chpn", start_map, c_blocks, precision=HIGH)
    shard_pull = jnp.sum(jnp.exp(prefix_log)[:, :, None, None] * local_pull, axis=0)

    leaving = exclusive_scan(shard_decay, shard_pull, "ctx", -1)
    running = leaving
    block_exit = [None] * blocks
    for index in reversed(range(blocks)):
        block_exit[index] = running
        running = block_decay[index][:, None, None] * running + local_pull[index]
    block_exit = jnp.stack(block_exit)

    b_exit = jnp.einsum("csn,chpn->cshp", b_blocks, block_exit, precision=HIGH)
    pulled = (
        jnp.einsum("ctsh,cthp->cshp", weighted, grad_blocks, precision=HIGH)
        + tail_decay[..., None] * b_exit
    )
    grad_x_blocks = d_blocks[..., None] * pulled
    grad_step_blocks = jnp.sum(x_blocks * pulled, axis=3)
    pair_grad = jnp.einsum("cthp,cshp->ctsh", grad_blocks, x_blocks, precision=HIGH)
    masked = pair_grad * decay_map * d_blocks[:, None, :, :]
    grad_scores = jnp.sum(masked, axis=3)
    grad_c_blocks = jnp.einsum("cts,csn->ctn", grad_scores, b_blocks, precision=HIGH)
    grad_b_blocks = jnp.einsum("cts,ctn->csn", grad_scores, c_blocks, precision=HIGH)
    through = masked * scores[..., None]
    grad_cum = jnp.sum(through, axis=2) - jnp.sum(through, axis=1)
    grad_cum = grad_cum + jnp.sum(start_map * carried_raw, axis=3)
    grad_c_blocks = grad_c_blocks + jnp.einsum(
        "cthp,chpn->ctn", start_map, block_entry, precision=HIGH
    )
    release = tail_weight * jnp.sum(x_blocks * b_exit, axis=3)
    grad_cum = grad_cum - release
    end_total = jnp.sum(release, axis=1) + jnp.exp(block_ends) * jnp.sum(
        block_entry * block_exit, axis=(2, 3)
    )
    grad_cum = jnp.concatenate(
        [grad_cum[:, :-1], grad_cum[:, -1:] + end_total[:, None, :]], axis=1
    )
    grad_log_blocks = jnp.flip(jnp.cumsum(jnp.flip(grad_cum, 1), axis=1), 1)
    grad_b_blocks = grad_b_blocks + jnp.einsum(
        "cshp,chpn->csn", tail_weight[..., None] * x_blocks, block_exit, precision=HIGH
    )

    grad_log_rows = grad_log_blocks.reshape(length, head_count)
    grad_step_rows = (
        grad_step_blocks.reshape(length, head_count) - decay_rate[None, :] * grad_log_rows
    )
    grad_alog_part = decay_rate * -jnp.sum(step_size * grad_log_rows, axis=0)
    grad_dt = (grad_step_rows * jax.nn.sigmoid(dt_raw).T).T
    grad_x_act = grad_x_blocks.reshape(length, row_width) + skip_rep[None, :] * grad_ssm
    grad_bc_act = jnp.concatenate(
        [grad_b_blocks.reshape(length, state_dim), grad_c_blocks.reshape(length, state_dim)], axis=1
    )
    grad_x_pre = grad_x_act * silu_grad(x_pre)
    grad_bc_pre = grad_bc_act * silu_grad(bc_pre)
    ahead = passed_along(
        jnp.concatenate([grad_x_pre[: tap_count - 1], grad_bc_pre[: tap_count - 1]], axis=1),
        "ctx",
        -1,
    )
    x_ahead = jnp.concatenate([grad_x_pre, ahead[:, :row_width]], axis=0)
    bc_ahead = jnp.concatenate([grad_bc_pre, ahead[:, row_width:]], axis=0)
    grad_x = back_taps(x_ahead, conv_x, length).astype(jnp.bfloat16)
    bc_back = back_taps(bc_ahead, conv_bc, length)
    grad_convx_part = weight_taps(grad_x_pre, x_padded, length, tap_count)
    grad_convbc_part = weight_taps(grad_bc_pre, bc_padded, length, tap_count)
    per_head = jnp.concatenate(
        [grad_alog_part, grad_skip_part, grad_convx_part.reshape(-1), grad_gain_part]
    )
    totals = all_sum(jnp.concatenate([per_head, grad_convbc_part.reshape(-1)]), "ctx")
    per_size = per_head.shape[0]
    shares, convbc_total = sum_scatter(bc_back, totals[per_size:], "head")
    grad_b = shares[:, :state_dim].astype(jnp.bfloat16)
    grad_c = shares[:, state_dim:].astype(jnp.bfloat16)
    grad_alog = totals[:head_count]
    grad_dskip = totals[head_count : 2 * head_count]
    convx_size = grad_convx_part.size
    grad_convx = totals[2 * head_count : 2 * head_count + convx_size].reshape(
        grad_convx_part.shape
    )
    grad_gain = totals[2 * head_count + convx_size : per_size]
    grad_convbc = convbc_total.reshape(grad_convbc_part.shape)
    return (
        y_out,
        grad_x,
        grad_z,
        grad_b,
        grad_c,
        grad_dt,
        grad_alog,
        grad_dskip,
        grad_convx,
        grad_convbc,
        grad_gain,
    )


def solution(mesh):
    return jax.shard_map(
        local,
        mesh=mesh,
        in_specs=(
            P("ctx", "head"),
            P("ctx", "head"),
            P("ctx", None),
            P("ctx", None),
            P("head", "ctx"),
            P("head"),
            P("head"),
            P(None, "head"),
            P(),
            P("head"),
            P("ctx", "head"),
        ),
        out_specs=(
            P("ctx", "head"),
            P("ctx", "head"),
            P("ctx", "head"),
            P(("ctx", "head"), None),
            P(("ctx", "head"), None),
            P("head", "ctx"),
            P("head"),
            P("head"),
            P(None, "head"),
            P(),
            P("head"),
        ),
        check_vma=False,
    )
```

```python
import jax
import jax.numpy as jnp
from jax import lax
from jax.sharding import PartitionSpec as P

HEADS = 128
HEAD_DIM = 64
GROUP = 256


HIGH = lax.Precision.HIGHEST
EPS = 1e-05


def passed_along(block, axis, distance):
    devices = range(lax.axis_size(axis))
    route = [(i - distance, i) for i in devices if i - distance in devices]
    return lax.ppermute(block, axis, route)


def exclusive_scan(decay, state, axis, direction):
    count = lax.axis_size(axis)
    rows = state.shape[1]
    half = state.shape[0] // 2

    def packed(decay_part, state_part):
        decay_row = jnp.broadcast_to(decay_part[:, None, None], state_part[:, :1].shape)
        return jnp.concatenate([state_part, decay_row], axis=1)

    def unpacked(part):
        return part[:, rows, 0], part[:, :rows]

    first = 0 if direction > 0 else 1
    second = 1 - first
    pairs = count // 2
    swap = [(2 * pair + core, 2 * pair + 1 - core) for pair in range(pairs) for core in (0, 1)]
    other_decay, other_state = unpacked(lax.ppermute(packed(decay, state), axis, swap))
    core = lax.axis_index(axis) % 2
    is_second = core == second
    front_decay = jnp.where(is_second, other_decay, decay)
    front_state = jnp.where(is_second, other_state, state)
    rear_decay = jnp.where(is_second, decay, other_decay)
    rear_state = jnp.where(is_second, state, other_state)
    inc_state = lax.dynamic_slice_in_dim(
        rear_decay[:, None, None] * front_state + rear_state, core * half, half, axis=0
    )
    inc_decay = lax.dynamic_slice_in_dim(rear_decay * front_decay, core * half, half, axis=0)
    exc_decay = jnp.ones_like(inc_decay)
    exc_state = jnp.zeros_like(inc_state)
    distance = 1
    while distance < pairs:
        route = [
            (2 * pair + lane, 2 * (pair + distance * direction) + lane)
            for pair in range(pairs)
            for lane in (0, 1)
            if 0 <= pair + distance * direction < pairs
        ]
        got_decay, got_state = unpacked(
            lax.ppermute(packed(inc_decay, inc_state), axis, route)
        )
        exc_state = exc_state + exc_decay[:, None, None] * got_state
        exc_decay = exc_decay * got_decay
        if 2 * distance < pairs:
            inc_state = inc_state + inc_decay[:, None, None] * got_state
            inc_decay = inc_decay * got_decay
        distance *= 2
    other_half = lax.ppermute(exc_state, axis, swap)
    entering = jnp.where(
        core == 0,
        jnp.concatenate([exc_state, other_half], axis=0),
        jnp.concatenate([other_half, exc_state], axis=0),
    )
    return jnp.where(is_second, front_decay[:, None, None] * entering + front_state, entering)


def digit_plan(count):
    plan = []
    stride = 1
    while stride < count:
        radix = 4 if (count // stride) % 4 == 0 else 2
        plan.append((stride, radix))
        stride *= radix
    return plan


def shifted(block, axis, stride, radix, shift):
    route = []
    for source in range(lax.axis_size(axis)):
        digit = (source // stride) % radix
        route.append((source, source + ((digit + shift) % radix - digit) * stride))
    return lax.ppermute(block, axis, route)


def all_sum(block, axis):
    for stride, radix in digit_plan(lax.axis_size(axis)):
        got = [block] + [shifted(block, axis, stride, radix, shift) for shift in range(1, radix)]
        digit = (lax.axis_index(axis) // stride) % radix
        ordered = jnp.take(jnp.stack(got), (digit - jnp.arange(radix)) % radix, axis=0)
        block = ordered[0]
        for index in range(1, radix):
            block = block + ordered[index]
    return block


def sum_scatter(block, extra, axis):
    count = lax.axis_size(axis)
    plan = digit_plan(count)
    trailing = block.ndim - 1
    chunk = block.shape[0] // count
    block = block.reshape(tuple(radix for _, radix in reversed(plan)) + (chunk,) + block.shape[1:])
    for stride, radix in plan:
        digit = (lax.axis_index(axis) // stride) % radix
        where = block.ndim - 2 - trailing
        total = lax.dynamic_index_in_dim(block, digit, axis=where, keepdims=False)
        size = total.size
        extras = [extra]
        for shift in range(1, radix):
            part = lax.dynamic_index_in_dim(block, (digit + shift) % radix, axis=where, keepdims=False)
            got = shifted(jnp.concatenate([part.reshape(-1), extra]), axis, stride, radix, shift)
            total = total + got[:size].reshape(total.shape)
            extras.append(got[size:])
        ordered = jnp.take(jnp.stack(extras), (digit - jnp.arange(radix)) % radix, axis=0)
        extra = ordered[0]
        for index in range(1, radix):
            extra = extra + ordered[index]
        block = total
    return block, extra


def silu_grad(value):
    sigma = jax.nn.sigmoid(value)
    return sigma * (1.0 + value * (1.0 - sigma))


def tap_sum(padded, weight, count):
    summed = jnp.zeros((count, padded.shape[1]), jnp.float32)
    for offset in range(weight.shape[0]):
        summed = summed + weight[offset][None, :] * padded[offset : offset + count].astype(
            jnp.float32
        )
    return summed


def back_taps(ahead, weight, count):
    final_tap = weight.shape[0] - 1
    summed = jnp.zeros((count, ahead.shape[1]), jnp.float32)
    for offset in range(weight.shape[0]):
        summed = (
            summed
            + weight[offset][None, :] * ahead[final_tap - offset : final_tap - offset + count]
        )
    return summed


def weight_taps(grad_pre, padded, count, tap_count):
    return jnp.stack(
        [
            jnp.sum(grad_pre * padded[offset : offset + count].astype(jnp.float32), axis=0)
            for offset in range(tap_count)
        ]
    )


def decay_table(cum_blocks):
    size_rows = cum_blocks.shape[1]
    row_ids = lax.broadcasted_iota(jnp.int32, (size_rows, size_rows), 0)
    col_ids = lax.broadcasted_iota(jnp.int32, (size_rows, size_rows), 1)
    allowed = (col_ids <= row_ids)[None, :, :, None]
    spread = cum_blocks[:, :, None, :] - cum_blocks[:, None, :, :]
    return jnp.where(allowed, jnp.exp(jnp.where(allowed, spread, 0.0)), 0.0)


def local(
    x_proj, z_proj, b_proj, c_proj, dt_raw, a_log, d_skip, conv_x, conv_bc, norm_gain, grad_out
):
    length = x_proj.shape[0]
    head_count = dt_raw.shape[0]
    row_width = x_proj.shape[1]
    head_dim = row_width // head_count
    state_dim = b_proj.shape[1]
    tap_count = conv_x.shape[0]
    blocks = length // GROUP
    channels = HEADS * HEAD_DIM
    bc_proj = jnp.concatenate([b_proj, c_proj], axis=1)
    edges = passed_along(
        jnp.concatenate(
            [x_proj[length - tap_count + 1 :], bc_proj[length - tap_count + 1 :]], axis=1
        ),
        "ctx",
        1,
    )
    x_padded = jnp.concatenate([edges[:, :row_width], x_proj], axis=0)
    bc_padded = jnp.concatenate([edges[:, row_width:], bc_proj], axis=0)
    x_pre = tap_sum(x_padded, conv_x, length)
    bc_pre = tap_sum(bc_padded, conv_bc, length)
    x_act = jax.nn.silu(x_pre)
    bc_act = jax.nn.silu(bc_pre)
    decay_rate = jnp.exp(a_log)
    step_size = jax.nn.softplus(dt_raw).T
    x_blocks = x_act.reshape(blocks, GROUP, head_count, head_dim)
    b_blocks = bc_act[:, :state_dim].reshape(blocks, GROUP, state_dim)
    c_blocks = bc_act[:, state_dim:].reshape(blocks, GROUP, state_dim)
    d_blocks = step_size.reshape(blocks, GROUP, head_count)
    cum_blocks = jnp.cumsum(
        (-step_size * decay_rate[None, :]).reshape(blocks, GROUP, head_count), axis=1
    )
    block_ends = cum_blocks[:, -1, :]
    block_decay = jnp.exp(block_ends)
    tail_decay = jnp.exp(cum_blocks[:, -1:, :] - cum_blocks)
    tail_weight = tail_decay * d_blocks
    block_states = jnp.einsum(
        "cshp,csn->chpn", tail_weight[..., None] * x_blocks, b_blocks, precision=HIGH
    )

    running = jnp.zeros((head_count, head_dim, state_dim), jnp.float32)
    local_entering = []
    for index in range(blocks):
        local_entering.append(running)
        running = block_decay[index][:, None, None] * running + block_states[index]
    shard_state = running
    local_entering = jnp.stack(local_entering)
    prefix_log = jnp.cumsum(block_ends, axis=0) - block_ends
    shard_decay = jnp.exp(jnp.sum(block_ends, axis=0))

    entering = exclusive_scan(shard_decay, shard_state, "ctx", 1)
    block_entry = jnp.exp(prefix_log)[:, :, None, None] * entering[None] + local_entering

    decay_map = decay_table(cum_blocks)
    scores = jnp.einsum("ctn,csn->cts", c_blocks, b_blocks, precision=HIGH)
    weighted = scores[..., None] * decay_map
    mixing = weighted * d_blocks[:, None, :, :]
    inside = jnp.einsum("ctsh,cshp->cthp", mixing, x_blocks, precision=HIGH)
    carried_raw = jnp.einsum("ctn,chpn->cthp", c_blocks, block_entry, precision=HIGH)
    start_decay = jnp.exp(cum_blocks)
    ssm_blocks = inside + start_decay[..., None] * carried_raw
    skip_rep = jnp.repeat(d_skip, head_dim)
    ssm_out = ssm_blocks.reshape(length, row_width) + skip_rep[None, :] * x_act
    z_float = z_proj.astype(jnp.float32)
    gate_act = jax.nn.silu(z_float)
    gated_out = ssm_out * gate_act
    grad_float = grad_out.astype(jnp.float32)
    scaled_grad = norm_gain[None, :] * grad_float
    norm_sums = all_sum(
        jnp.stack(
            [jnp.sum(gated_out * gated_out, axis=1), jnp.sum(scaled_grad * gated_out, axis=1)]
        ),
        "head",
    )
    square_sum, cross_sum = norm_sums[0], norm_sums[1]
    inv_rms = lax.rsqrt(square_sum / channels + EPS)[:, None]
    y_out = (gated_out * inv_rms * norm_gain[None, :]).astype(jnp.bfloat16)
    grad_gain_part = jnp.sum(grad_float * gated_out * inv_rms, axis=0)
    grad_gated = inv_rms * scaled_grad - gated_out * (inv_rms * inv_rms * inv_rms) * (
        cross_sum[:, None] / channels
    )
    grad_ssm = grad_gated * gate_act
    grad_z = (grad_gated * ssm_out * silu_grad(z_float)).astype(jnp.bfloat16)
    grad_skip_part = jnp.sum((grad_ssm * x_act).reshape(length, head_count, head_dim), axis=(0, 2))
    grad_blocks = grad_ssm.reshape(blocks, GROUP, head_count, head_dim)
    start_map = start_decay[..., None] * grad_blocks
    local_pull = jnp.einsum("cthp,ctn->chpn", start_map, c_blocks, precision=HIGH)
    shard_pull = jnp.sum(jnp.exp(prefix_log)[:, :, None, None] * local_pull, axis=0)

    leaving = exclusive_scan(shard_decay, shard_pull, "ctx", -1)
    running = leaving
    block_exit = [None] * blocks
    for index in reversed(range(blocks)):
        block_exit[index] = running
        running = block_decay[index][:, None, None] * running + local_pull[index]
    block_exit = jnp.stack(block_exit)

    b_exit = jnp.einsum("csn,chpn->cshp", b_blocks, block_exit, precision=HIGH)
    pulled = (
        jnp.einsum("ctsh,cthp->cshp", weighted, grad_blocks, precision=HIGH)
        + tail_decay[..., None] * b_exit
    )
    grad_x_blocks = d_blocks[..., None] * pulled
    grad_step_blocks = jnp.sum(x_blocks * pulled, axis=3)
    pair_grad = jnp.einsum("cthp,cshp->ctsh", grad_blocks, x_blocks, precision=HIGH)
    masked = pair_grad * decay_map * d_blocks[:, None, :, :]
    grad_scores = jnp.sum(masked, axis=3)
    grad_c_blocks = jnp.einsum("cts,csn->ctn", grad_scores, b_blocks, precision=HIGH)
    grad_b_blocks = jnp.einsum("cts,ctn->csn", grad_scores, c_blocks, precision=HIGH)
    through = masked * scores[..., None]
    grad_cum = jnp.sum(through, axis=2) - jnp.sum(through, axis=1)
    grad_cum = grad_cum + jnp.sum(start_map * carried_raw, axis=3)
    grad_c_blocks = grad_c_blocks + jnp.einsum(
        "cthp,chpn->ctn", start_map, block_entry, precision=HIGH
    )
    release = tail_weight * jnp.sum(x_blocks * b_exit, axis=3)
    grad_cum = grad_cum - release
    end_total = jnp.sum(release, axis=1) + jnp.exp(block_ends) * jnp.sum(
        block_entry * block_exit, axis=(2, 3)
    )
    grad_cum = jnp.concatenate(
        [grad_cum[:, :-1], grad_cum[:, -1:] + end_total[:, None, :]], axis=1
    )
    grad_log_blocks = jnp.flip(jnp.cumsum(jnp.flip(grad_cum, 1), axis=1), 1)
    grad_b_blocks = grad_b_blocks + jnp.einsum(
        "cshp,chpn->csn", tail_weight[..., None] * x_blocks, block_exit, precision=HIGH
    )

    grad_log_rows = grad_log_blocks.reshape(length, head_count)
    grad_step_rows = (
        grad_step_blocks.reshape(length, head_count) - decay_rate[None, :] * grad_log_rows
    )
    grad_alog_part = decay_rate * -jnp.sum(step_size * grad_log_rows, axis=0)
    grad_dt = (grad_step_rows * jax.nn.sigmoid(dt_raw).T).T
    grad_x_act = grad_x_blocks.reshape(length, row_width) + skip_rep[None, :] * grad_ssm
    grad_bc_act = jnp.concatenate(
        [grad_b_blocks.reshape(length, state_dim), grad_c_blocks.reshape(length, state_dim)], axis=1
    )
    grad_x_pre = grad_x_act * silu_grad(x_pre)
    grad_bc_pre = grad_bc_act * silu_grad(bc_pre)
    ahead = passed_along(
        jnp.concatenate([grad_x_pre[: tap_count - 1], grad_bc_pre[: tap_count - 1]], axis=1),
        "ctx",
        -1,
    )
    x_ahead = jnp.concatenate([grad_x_pre, ahead[:, :row_width]], axis=0)
    bc_ahead = jnp.concatenate([grad_bc_pre, ahead[:, row_width:]], axis=0)
    grad_x = back_taps(x_ahead, conv_x, length).astype(jnp.bfloat16)
    bc_back = back_taps(bc_ahead, conv_bc, length)
    grad_convx_part = weight_taps(grad_x_pre, x_padded, length, tap_count)
    grad_convbc_part = weight_taps(grad_bc_pre, bc_padded, length, tap_count)
    per_head = jnp.concatenate(
        [grad_alog_part, grad_skip_part, grad_convx_part.reshape(-1), grad_gain_part]
    )
    totals = all_sum(jnp.concatenate([per_head, grad_convbc_part.reshape(-1)]), "ctx")
    per_size = per_head.shape[0]
    shares, convbc_total = sum_scatter(bc_back, totals[per_size:], "head")
    grad_b = shares[:, :state_dim].astype(jnp.bfloat16)
    grad_c = shares[:, state_dim:].astype(jnp.bfloat16)
    grad_alog = totals[:head_count]
    grad_dskip = totals[head_count : 2 * head_count]
    convx_size = grad_convx_part.size
    grad_convx = totals[2 * head_count : 2 * head_count + convx_size].reshape(
        grad_convx_part.shape
    )
    grad_gain = totals[2 * head_count + convx_size : per_size]
    grad_convbc = convbc_total.reshape(grad_convbc_part.shape)
    return (
        y_out,
        grad_x,
        grad_z,
        grad_b,
        grad_c,
        grad_dt,
        grad_alog,
        grad_dskip,
        grad_convx,
        grad_convbc,
        grad_gain,
    )


def solution(mesh):
    return jax.shard_map(
        local,
        mesh=mesh,
        in_specs=(
            P("ctx", "head"),
            P("ctx", "head"),
            P("ctx", None),
            P("ctx", None),
            P("head", "ctx"),
            P("head"),
            P("head"),
            P(None, "head"),
            P(),
            P("head"),
            P("ctx", "head"),
        ),
        out_specs=(
            P("ctx", "head"),
            P("ctx", "head"),
            P("ctx", "head"),
            P(("ctx", "head"), None),
            P(("ctx", "head"), None),
            P("head", "ctx"),
            P("head"),
            P("head"),
            P(None, "head"),
            P(),
            P("head"),
        ),
        check_vma=False,
    )
```

```python
import jax
import jax.numpy as jnp
from jax import lax
from jax.sharding import PartitionSpec as P

HEADS = 128
HEAD_DIM = 64
GROUP = 256


HIGH = lax.Precision.HIGHEST
EPS = 1e-05


def passed_along(block, axis, distance):
    devices = range(lax.axis_size(axis))
    route = [(i - distance, i) for i in devices if i - distance in devices]
    return lax.ppermute(block, axis, route)


def exclusive_scan(decay, state, axis, direction):
    count = lax.axis_size(axis)
    rows = state.shape[1]
    half = state.shape[0] // 2

    def packed(decay_part, state_part):
        decay_row = jnp.broadcast_to(decay_part[:, None, None], state_part[:, :1].shape)
        return jnp.concatenate([state_part, decay_row], axis=1)

    def unpacked(part):
        return part[:, rows, 0], part[:, :rows]

    first = 0 if direction > 0 else 1
    second = 1 - first
    pairs = count // 2
    swap = [(2 * pair + core, 2 * pair + 1 - core) for pair in range(pairs) for core in (0, 1)]
    other_decay, other_state = unpacked(lax.ppermute(packed(decay, state), axis, swap))
    core = lax.axis_index(axis) % 2
    is_second = core == second
    front_decay = jnp.where(is_second, other_decay, decay)
    front_state = jnp.where(is_second, other_state, state)
    rear_decay = jnp.where(is_second, decay, other_decay)
    rear_state = jnp.where(is_second, state, other_state)
    inc_state = lax.dynamic_slice_in_dim(
        rear_decay[:, None, None] * front_state + rear_state, core * half, half, axis=0
    )
    inc_decay = lax.dynamic_slice_in_dim(rear_decay * front_decay, core * half, half, axis=0)
    exc_decay = jnp.ones_like(inc_decay)
    exc_state = jnp.zeros_like(inc_state)
    plan = digit_plan(pairs)
    for index, (stride, radix) in enumerate(plan):
        got = []
        for shift in range(1, radix):
            step = stride * shift * direction
            route = [
                (2 * pair + lane, 2 * (pair + step) + lane)
                for pair in range(pairs)
                for lane in (0, 1)
                if 0 <= pair + step < pairs
            ]
            got.append(unpacked(lax.ppermute(packed(inc_decay, inc_state), axis, route)))
        for got_decay, got_state in got:
            exc_state = exc_state + exc_decay[:, None, None] * got_state
            exc_decay = exc_decay * got_decay
        if index + 1 < len(plan):
            for got_decay, got_state in got:
                inc_state = inc_state + inc_decay[:, None, None] * got_state
                inc_decay = inc_decay * got_decay
    other_half = lax.ppermute(exc_state, axis, swap)
    entering = jnp.where(
        core == 0,
        jnp.concatenate([exc_state, other_half], axis=0),
        jnp.concatenate([other_half, exc_state], axis=0),
    )
    return jnp.where(is_second, front_decay[:, None, None] * entering + front_state, entering)


def digit_plan(count):
    plan = []
    stride = 1
    while stride < count:
        radix = 4 if (count // stride) % 4 == 0 else 2
        plan.append((stride, radix))
        stride *= radix
    return plan


def shifted(block, axis, stride, radix, shift):
    route = []
    for source in range(lax.axis_size(axis)):
        digit = (source // stride) % radix
        route.append((source, source + ((digit + shift) % radix - digit) * stride))
    return lax.ppermute(block, axis, route)


def all_sum(block, axis):
    for stride, radix in digit_plan(lax.axis_size(axis)):
        got = [block] + [shifted(block, axis, stride, radix, shift) for shift in range(1, radix)]
        digit = (lax.axis_index(axis) // stride) % radix
        ordered = jnp.take(jnp.stack(got), (digit - jnp.arange(radix)) % radix, axis=0)
        block = ordered[0]
        for index in range(1, radix):
            block = block + ordered[index]
    return block


def sum_scatter(block, extra, axis):
    count = lax.axis_size(axis)
    plan = digit_plan(count)
    trailing = block.ndim - 1
    chunk = block.shape[0] // count
    block = block.reshape(tuple(radix for _, radix in reversed(plan)) + (chunk,) + block.shape[1:])
    for stride, radix in plan:
        digit = (lax.axis_index(axis) // stride) % radix
        where = block.ndim - 2 - trailing
        total = lax.dynamic_index_in_dim(block, digit, axis=where, keepdims=False)
        size = total.size
        extras = [extra]
        for shift in range(1, radix):
            part = lax.dynamic_index_in_dim(block, (digit + shift) % radix, axis=where, keepdims=False)
            got = shifted(jnp.concatenate([part.reshape(-1), extra]), axis, stride, radix, shift)
            total = total + got[:size].reshape(total.shape)
            extras.append(got[size:])
        ordered = jnp.take(jnp.stack(extras), (digit - jnp.arange(radix)) % radix, axis=0)
        extra = ordered[0]
        for index in range(1, radix):
            extra = extra + ordered[index]
        block = total
    return block, extra


def silu_grad(value):
    sigma = jax.nn.sigmoid(value)
    return sigma * (1.0 + value * (1.0 - sigma))


def tap_sum(padded, weight, count):
    summed = jnp.zeros((count, padded.shape[1]), jnp.float32)
    for offset in range(weight.shape[0]):
        summed = summed + weight[offset][None, :] * padded[offset : offset + count].astype(
            jnp.float32
        )
    return summed


def back_taps(ahead, weight, count):
    final_tap = weight.shape[0] - 1
    summed = jnp.zeros((count, ahead.shape[1]), jnp.float32)
    for offset in range(weight.shape[0]):
        summed = (
            summed
            + weight[offset][None, :] * ahead[final_tap - offset : final_tap - offset + count]
        )
    return summed


def weight_taps(grad_pre, padded, count, tap_count):
    return jnp.stack(
        [
            jnp.sum(grad_pre * padded[offset : offset + count].astype(jnp.float32), axis=0)
            for offset in range(tap_count)
        ]
    )


def decay_table(cum_blocks):
    size_rows = cum_blocks.shape[1]
    row_ids = lax.broadcasted_iota(jnp.int32, (size_rows, size_rows), 0)
    col_ids = lax.broadcasted_iota(jnp.int32, (size_rows, size_rows), 1)
    allowed = (col_ids <= row_ids)[None, :, :, None]
    spread = cum_blocks[:, :, None, :] - cum_blocks[:, None, :, :]
    return jnp.where(allowed, jnp.exp(jnp.where(allowed, spread, 0.0)), 0.0)


def local(
    x_proj, z_proj, b_proj, c_proj, dt_raw, a_log, d_skip, conv_x, conv_bc, norm_gain, grad_out
):
    length = x_proj.shape[0]
    head_count = dt_raw.shape[0]
    row_width = x_proj.shape[1]
    head_dim = row_width // head_count
    state_dim = b_proj.shape[1]
    tap_count = conv_x.shape[0]
    blocks = length // GROUP
    channels = HEADS * HEAD_DIM
    bc_proj = jnp.concatenate([b_proj, c_proj], axis=1)
    edges = passed_along(
        jnp.concatenate(
            [x_proj[length - tap_count + 1 :], bc_proj[length - tap_count + 1 :]], axis=1
        ),
        "ctx",
        1,
    )
    x_padded = jnp.concatenate([edges[:, :row_width], x_proj], axis=0)
    bc_padded = jnp.concatenate([edges[:, row_width:], bc_proj], axis=0)
    x_pre = tap_sum(x_padded, conv_x, length)
    bc_pre = tap_sum(bc_padded, conv_bc, length)
    x_act = jax.nn.silu(x_pre)
    bc_act = jax.nn.silu(bc_pre)
    decay_rate = jnp.exp(a_log)
    step_size = jax.nn.softplus(dt_raw).T
    x_blocks = x_act.reshape(blocks, GROUP, head_count, head_dim)
    b_blocks = bc_act[:, :state_dim].reshape(blocks, GROUP, state_dim)
    c_blocks = bc_act[:, state_dim:].reshape(blocks, GROUP, state_dim)
    d_blocks = step_size.reshape(blocks, GROUP, head_count)
    cum_blocks = jnp.cumsum(
        (-step_size * decay_rate[None, :]).reshape(blocks, GROUP, head_count), axis=1
    )
    block_ends = cum_blocks[:, -1, :]
    block_decay = jnp.exp(block_ends)
    tail_decay = jnp.exp(cum_blocks[:, -1:, :] - cum_blocks)
    tail_weight = tail_decay * d_blocks
    block_states = jnp.einsum(
        "cshp,csn->chpn", tail_weight[..., None] * x_blocks, b_blocks, precision=HIGH
    )

    running = jnp.zeros((head_count, head_dim, state_dim), jnp.float32)
    local_entering = []
    for index in range(blocks):
        local_entering.append(running)
        running = block_decay[index][:, None, None] * running + block_states[index]
    shard_state = running
    local_entering = jnp.stack(local_entering)
    prefix_log = jnp.cumsum(block_ends, axis=0) - block_ends
    shard_decay = jnp.exp(jnp.sum(block_ends, axis=0))

    entering = exclusive_scan(shard_decay, shard_state, "ctx", 1)
    block_entry = jnp.exp(prefix_log)[:, :, None, None] * entering[None] + local_entering

    decay_map = decay_table(cum_blocks)
    scores = jnp.einsum("ctn,csn->cts", c_blocks, b_blocks, precision=HIGH)
    weighted = scores[..., None] * decay_map
    mixing = weighted * d_blocks[:, None, :, :]
    inside = jnp.einsum("ctsh,cshp->cthp", mixing, x_blocks, precision=HIGH)
    carried_raw = jnp.einsum("ctn,chpn->cthp", c_blocks, block_entry, precision=HIGH)
    start_decay = jnp.exp(cum_blocks)
    ssm_blocks = inside + start_decay[..., None] * carried_raw
    skip_rep = jnp.repeat(d_skip, head_dim)
    ssm_out = ssm_blocks.reshape(length, row_width) + skip_rep[None, :] * x_act
    z_float = z_proj.astype(jnp.float32)
    gate_act = jax.nn.silu(z_float)
    gated_out = ssm_out * gate_act
    grad_float = grad_out.astype(jnp.float32)
    scaled_grad = norm_gain[None, :] * grad_float
    norm_sums = all_sum(
        jnp.stack(
            [jnp.sum(gated_out * gated_out, axis=1), jnp.sum(scaled_grad * gated_out, axis=1)]
        ),
        "head",
    )
    square_sum, cross_sum = norm_sums[0], norm_sums[1]
    inv_rms = lax.rsqrt(square_sum / channels + EPS)[:, None]
    y_out = (gated_out * inv_rms * norm_gain[None, :]).astype(jnp.bfloat16)
    grad_gain_part = jnp.sum(grad_float * gated_out * inv_rms, axis=0)
    grad_gated = inv_rms * scaled_grad - gated_out * (inv_rms * inv_rms * inv_rms) * (
        cross_sum[:, None] / channels
    )
    grad_ssm = grad_gated * gate_act
    grad_z = (grad_gated * ssm_out * silu_grad(z_float)).astype(jnp.bfloat16)
    grad_skip_part = jnp.sum((grad_ssm * x_act).reshape(length, head_count, head_dim), axis=(0, 2))
    grad_blocks = grad_ssm.reshape(blocks, GROUP, head_count, head_dim)
    start_map = start_decay[..., None] * grad_blocks
    local_pull = jnp.einsum("cthp,ctn->chpn", start_map, c_blocks, precision=HIGH)
    shard_pull = jnp.sum(jnp.exp(prefix_log)[:, :, None, None] * local_pull, axis=0)

    leaving = exclusive_scan(shard_decay, shard_pull, "ctx", -1)
    running = leaving
    block_exit = [None] * blocks
    for index in reversed(range(blocks)):
        block_exit[index] = running
        running = block_decay[index][:, None, None] * running + local_pull[index]
    block_exit = jnp.stack(block_exit)

    b_exit = jnp.einsum("csn,chpn->cshp", b_blocks, block_exit, precision=HIGH)
    pulled = (
        jnp.einsum("ctsh,cthp->cshp", weighted, grad_blocks, precision=HIGH)
        + tail_decay[..., None] * b_exit
    )
    grad_x_blocks = d_blocks[..., None] * pulled
    grad_step_blocks = jnp.sum(x_blocks * pulled, axis=3)
    pair_grad = jnp.einsum("cthp,cshp->ctsh", grad_blocks, x_blocks, precision=HIGH)
    masked = pair_grad * decay_map * d_blocks[:, None, :, :]
    grad_scores = jnp.sum(masked, axis=3)
    grad_c_blocks = jnp.einsum("cts,csn->ctn", grad_scores, b_blocks, precision=HIGH)
    grad_b_blocks = jnp.einsum("cts,ctn->csn", grad_scores, c_blocks, precision=HIGH)
    through = masked * scores[..., None]
    grad_cum = jnp.sum(through, axis=2) - jnp.sum(through, axis=1)
    grad_cum = grad_cum + jnp.sum(start_map * carried_raw, axis=3)
    grad_c_blocks = grad_c_blocks + jnp.einsum(
        "cthp,chpn->ctn", start_map, block_entry, precision=HIGH
    )
    release = tail_weight * jnp.sum(x_blocks * b_exit, axis=3)
    grad_cum = grad_cum - release
    end_total = jnp.sum(release, axis=1) + jnp.exp(block_ends) * jnp.sum(
        block_entry * block_exit, axis=(2, 3)
    )
    grad_cum = jnp.concatenate(
        [grad_cum[:, :-1], grad_cum[:, -1:] + end_total[:, None, :]], axis=1
    )
    grad_log_blocks = jnp.flip(jnp.cumsum(jnp.flip(grad_cum, 1), axis=1), 1)
    grad_b_blocks = grad_b_blocks + jnp.einsum(
        "cshp,chpn->csn", tail_weight[..., None] * x_blocks, block_exit, precision=HIGH
    )

    grad_log_rows = grad_log_blocks.reshape(length, head_count)
    grad_step_rows = (
        grad_step_blocks.reshape(length, head_count) - decay_rate[None, :] * grad_log_rows
    )
    grad_alog_part = decay_rate * -jnp.sum(step_size * grad_log_rows, axis=0)
    grad_dt = (grad_step_rows * jax.nn.sigmoid(dt_raw).T).T
    grad_x_act = grad_x_blocks.reshape(length, row_width) + skip_rep[None, :] * grad_ssm
    grad_bc_act = jnp.concatenate(
        [grad_b_blocks.reshape(length, state_dim), grad_c_blocks.reshape(length, state_dim)], axis=1
    )
    grad_x_pre = grad_x_act * silu_grad(x_pre)
    grad_bc_pre = grad_bc_act * silu_grad(bc_pre)
    ahead = passed_along(
        jnp.concatenate([grad_x_pre[: tap_count - 1], grad_bc_pre[: tap_count - 1]], axis=1),
        "ctx",
        -1,
    )
    x_ahead = jnp.concatenate([grad_x_pre, ahead[:, :row_width]], axis=0)
    bc_ahead = jnp.concatenate([grad_bc_pre, ahead[:, row_width:]], axis=0)
    grad_x = back_taps(x_ahead, conv_x, length).astype(jnp.bfloat16)
    bc_back = back_taps(bc_ahead, conv_bc, length)
    grad_convx_part = weight_taps(grad_x_pre, x_padded, length, tap_count)
    grad_convbc_part = weight_taps(grad_bc_pre, bc_padded, length, tap_count)
    per_head = jnp.concatenate(
        [grad_alog_part, grad_skip_part, grad_convx_part.reshape(-1), grad_gain_part]
    )
    totals = all_sum(jnp.concatenate([per_head, grad_convbc_part.reshape(-1)]), "ctx")
    per_size = per_head.shape[0]
    shares, convbc_total = sum_scatter(bc_back, totals[per_size:], "head")
    grad_b = shares[:, :state_dim].astype(jnp.bfloat16)
    grad_c = shares[:, state_dim:].astype(jnp.bfloat16)
    grad_alog = totals[:head_count]
    grad_dskip = totals[head_count : 2 * head_count]
    convx_size = grad_convx_part.size
    grad_convx = totals[2 * head_count : 2 * head_count + convx_size].reshape(
        grad_convx_part.shape
    )
    grad_gain = totals[2 * head_count + convx_size : per_size]
    grad_convbc = convbc_total.reshape(grad_convbc_part.shape)
    return (
        y_out,
        grad_x,
        grad_z,
        grad_b,
        grad_c,
        grad_dt,
        grad_alog,
        grad_dskip,
        grad_convx,
        grad_convbc,
        grad_gain,
    )


def solution(mesh):
    return jax.shard_map(
        local,
        mesh=mesh,
        in_specs=(
            P("ctx", "head"),
            P("ctx", "head"),
            P("ctx", None),
            P("ctx", None),
            P("head", "ctx"),
            P("head"),
            P("head"),
            P(None, "head"),
            P(),
            P("head"),
            P("ctx", "head"),
        ),
        out_specs=(
            P("ctx", "head"),
            P("ctx", "head"),
            P("ctx", "head"),
            P(("ctx", "head"), None),
            P(("ctx", "head"), None),
            P("head", "ctx"),
            P("head"),
            P("head"),
            P(None, "head"),
            P(),
            P("head"),
        ),
        check_vma=False,
    )
```
